128 devices in a mesh: wide: 16 (over z, y), col: 8 (over x, core).
Axes of the slice: x: 4, y: 4, z: 4, core: 2. Of those that a mesh axis runs over, the one named last changes fastest.
Arguments:
- z_root: float32 [512, 16384], P('col', 'wide'), may hold values from -6 to 6
- z_child: float32 [512, 2, 8192], P('col', None, 'wide'), may hold values from -6 to 6
- z_grand: float32 [512, 4, 4096], P('col', None, 'wide'), may hold values from -6 to 6
- inv_root: float32 [16384, 16384], P('wide', 'col'), as said below
- inv_child: float32 [2, 8192, 8192], P(None, 'wide', 'col'), as said below
- inv_grand: float32 [4, 4096, 4096], P(None, 'wide', 'col'), as said below
- panel_child: float32 [2, 4096, 8192], P(None, 'col', 'wide'), may hold values from -0.046875 to 0.046875
- panel_grand: float32 [4, 2048, 4096], P(None, 'col', 'wide'), may hold values from -0.0625 to 0.0625
- anc_child: int32 [2, 32], P(None, 'col'), may hold values from 0 to 127, as said below
- anc_grand: int32 [4, 16], P(None, 'col'), may hold values from 0 to 255, as said below
Outputs:
- x_root: float32 [512, 16384], P('wide', 'col')
- x_child: float32 [512, 2, 8192], P('wide', None, 'col')
- x_grand: float32 [512, 4, 4096], P('wide', None, 'col')
The draws below stay inside these ranges and needn't reach their ends.
Inputs may be any that keep to these rules, and one draw needn't show every extreme that they name: inv_root is lower triangular with a positive diagonal (entries above the diagonal are zero). Each inv_child[k] is lower triangular with a positive diagonal. Each inv_grand[g] is lower triangular with a positive diagonal. `anc_child`: each row lists distinct blocks in rising order and always names block 0 and block 127. `anc_grand`: row g lists 2048 // 256 distinct root blocks in rising order, block 0 and block 127 among them, then as many distinct blocks of child g // 2 (numbered 16384 // 128 + (g // 2) * 64 onwards) in rising order, its first and its last among them.
All inputs are finite; a program needn't handle non-finite values.
Results may differ from the reference program's by a relative error of at most 0.000096.
Values sent between devices are 32-bit elements; how exact they have to be, the bound alone decides.
No kernel may reach another device: no remote copies, remote signals or barrier semaphores. Data moves between devices by JAX's collectives and lax.ppermute only.
A program may use at most 128 MiB of HBM per device.

```python
import math
import jax
import jax.numpy as jnp
from jax import lax

NR = 16384
NC = 8192
NG = 4096
KC = 2
KG = 4
ANC_C = 4096
ANC_G = 2048
BLK = 128
SAMPLES = 512


def lower_inverse(key, batch, span_size):
    key_lower, key_diagonal = jax.random.split(key)
    lower_part = jax.random.normal(key_lower, (batch, span_size, span_size), jnp.float32)
    diagonal = jax.random.uniform(key_diagonal, (batch, span_size), jnp.float32, 0.6, 1.6)
    row_index = lax.broadcasted_iota(jnp.int32, (span_size, span_size), 0)
    col_index = lax.broadcasted_iota(jnp.int32, (span_size, span_size), 1)
    below_mask = (row_index > col_index).astype(jnp.float32)
    on_diagonal = (row_index == col_index).astype(jnp.float32)
    scale = 0.7 / math.sqrt(span_size)
    return lower_part * below_mask[None] * scale + diagonal[:, :, None] * on_diagonal[None]


def draw_inv_root(key, part):
    return lower_inverse(jax.random.fold_in(key, 1), 1, NR)[0]


def draw_inv_child(key, part):
    return lower_inverse(jax.random.fold_in(key, 2), KC, NC)


def draw_inv_grand(key, part):
    return lower_inverse(jax.random.fold_in(key, 3), KG, NG)


def choose_blocks(key, first_block, block_total, kept_count):
    shuffled = jax.random.permutation(key, block_total - 2).astype(jnp.int32) + 1
    middle = jnp.sort(shuffled[:kept_count - 2])
    lowest = jnp.zeros((1,), jnp.int32)
    highest = jnp.full((1,), block_total - 1, jnp.int32)
    return jnp.concatenate([lowest, middle, highest]) + first_block


def draw_anc_child(key, part):
    listed = []
    for child in range(KC):
        listed.append(choose_blocks(jax.random.fold_in(key, 100 + child), 0, NR // BLK, ANC_C // BLK))
    return jnp.stack(listed)


def draw_anc_grand(key, part):
    listed = []
    half_count = ANC_G // BLK // 2
    for grand in range(KG):
        from_root = choose_blocks(jax.random.fold_in(key, 200 + grand), 0, NR // BLK, half_count)
        parent_start = NR // BLK + grand // 2 * (NC // BLK)
        from_parent = choose_blocks(jax.random.fold_in(key, 300 + grand), parent_start, NC // BLK, half_count)
        listed.append(jnp.concatenate([from_root, from_parent]))
    return jnp.stack(listed)


def shard_levels(key, extent, cuts, smallest, high):
    loudness = 1.0
    for dim, shards_of in cuts:
        steps = jax.random.uniform(jax.random.fold_in(jax.random.fold_in(key, 6), dim), (shards_of,), jnp.float32, smallest / len(cuts), high / len(cuts))
        loudness = loudness * jnp.repeat(jnp.exp(steps), extent[dim] // shards_of).reshape((-1,) + (1,) * (len(extent) - 1 - dim))
    return loudness


def gaussian(rng, extent, scale, most, cuts=(), kind=jnp.bfloat16):
    array = scale * jax.random.normal(rng, extent, jnp.float32)
    if cuts:
        array = array * shard_levels(rng, extent, cuts, -0.22, 0.18)
    return jnp.clip(array, -most, most).astype(kind)


def setup_inputs(seed: int = 0) -> dict:
    key_of = jax.random.split(jax.random.key(seed), 11)
    return {
        "z_root": gaussian(key_of[0], (SAMPLES, NR), 1.0, 6.0, ((0, 8), (1, 16)), jnp.float32),
        "z_child": gaussian(key_of[1], (SAMPLES, KC, NC), 1.0, 6.0, ((0, 8), (2, 16)), jnp.float32),
        "z_grand": gaussian(key_of[2], (SAMPLES, KG, NG), 1.0, 6.0, ((0, 8), (2, 16)), jnp.float32),
        "inv_root": draw_inv_root(jax.random.fold_in(key_of[10], 71), 0),
        "inv_child": draw_inv_child(jax.random.fold_in(key_of[10], 71), 0),
        "inv_grand": draw_inv_grand(jax.random.fold_in(key_of[10], 71), 0),
        "panel_child": gaussian(key_of[6], (KC, ANC_C, NC), (4 * ANC_C) ** -0.5, 0.046875, ((1, 8), (2, 16)), jnp.float32),
        "panel_grand": gaussian(key_of[7], (KG, ANC_G, NG), (4 * ANC_G) ** -0.5, 0.0625, ((1, 8), (2, 16)), jnp.float32),
        "anc_child": draw_anc_child(jax.random.fold_in(key_of[10], 71), 0),
        "anc_grand": draw_anc_grand(jax.random.fold_in(key_of[10], 71), 0),
    }


PRECISE = lax.Precision.HIGHEST


def block_rows(blocks):
    offsets = jnp.arange(BLK, dtype=jnp.int32)
    spread = blocks.astype(jnp.int32)[:, :, None] * BLK + offsets[None, None, :]
    return spread.reshape(blocks.shape[0], -1)


def reference(z_root, z_child, z_grand, inv_root, inv_child, inv_grand, panel_child, panel_grand, anc_child, anc_grand):
    x_root = jnp.dot(z_root, inv_root, precision=PRECISE, preferred_element_type=jnp.float32)
    near_rows = jnp.take(x_root, block_rows(anc_child).reshape(-1), axis=1).reshape(SAMPLES, KC, ANC_C)
    update_child = jnp.einsum("ska,kaj->skj", near_rows, panel_child, precision=PRECISE, preferred_element_type=jnp.float32)
    x_child = jnp.einsum("ski,kij->skj", z_child - update_child, inv_child, precision=PRECISE, preferred_element_type=jnp.float32)
    solved_all = jnp.concatenate([x_root, x_child.reshape(SAMPLES, KC * NC)], axis=1)
    far_rows = jnp.take(solved_all, block_rows(anc_grand).reshape(-1), axis=1).reshape(SAMPLES, KG, ANC_G)
    update_grand = jnp.einsum("sga,gaj->sgj", far_rows, panel_grand, precision=PRECISE, preferred_element_type=jnp.float32)
    x_grand = jnp.einsum("sgi,gij->sgj", z_grand - update_grand, inv_grand, precision=PRECISE, preferred_element_type=jnp.float32)
    return (x_root, x_child, x_grand)
```

```python
import jax
import jax.numpy as jnp
from jax import lax
from jax.sharding import PartitionSpec as P

BLK = 128


PRECISE = lax.Precision.HIGHEST


def pick_blocks(source_rows, blocks):
    leading = source_rows.shape[0]
    tiled = source_rows.reshape(leading, source_rows.shape[1] // BLK, BLK)
    selected = jnp.take(tiled, blocks.reshape(-1), axis=1)
    return selected.reshape(leading, blocks.shape[0], blocks.shape[1] * BLK)


def exchange_sum(partial, axis):
    n = lax.axis_size(axis)
    chunk = partial.shape[0] // n
    parts = lax.all_to_all(partial.reshape((n, chunk) + partial.shape[1:]), axis, 0, 0, tiled=False)
    return parts.sum(0)


def exchange_gather(local, axis, dim):
    n = lax.axis_size(axis)
    stacked = jnp.broadcast_to(local[None], (n,) + local.shape)
    parts = lax.all_to_all(stacked, axis, 0, 0, tiled=False)
    parts = jnp.moveaxis(parts, 0, dim)
    return parts.reshape(local.shape[:dim] + (n * local.shape[dim],) + local.shape[dim + 1 :])


def matmul(lhs, rhs, spec):
    return jnp.einsum(spec, lhs, rhs, precision=PRECISE, preferred_element_type=jnp.float32)


def level(z_local, update_partial, inverse):
    update = exchange_sum(update_partial, "col")
    right_side = exchange_gather(z_local - update, "col", 0)
    return exchange_sum(matmul(right_side, inverse, "ski,kij->skj"), "wide")


def per_device(
    z_root,
    z_child,
    z_grand,
    inv_root,
    inv_child,
    inv_grand,
    panel_child,
    panel_grand,
    anc_child,
    anc_grand,
):
    root_right = exchange_gather(z_root, "col", 0)
    x_root = exchange_sum(matmul(root_right, inv_root, "si,ij->sj"), "wide")
    root_rows = exchange_gather(x_root, "col", 1)
    near_rows = exchange_gather(pick_blocks(root_rows, anc_child), "wide", 0)
    x_child = level(z_child, matmul(near_rows, panel_child, "ska,kaj->skj"), inv_child)
    child_rows = exchange_gather(x_child, "col", 2)
    solved_all = jnp.concatenate([root_rows, child_rows.reshape(child_rows.shape[0], -1)], axis=1)
    far_rows = exchange_gather(pick_blocks(solved_all, anc_grand), "wide", 0)
    x_grand = level(z_grand, matmul(far_rows, panel_grand, "sga,gaj->sgj"), inv_grand)
    return (x_root, x_child, x_grand)


def solution(mesh):
    in_specs = (
        P("col", "wide"),
        P("col", None, "wide"),
        P("col", None, "wide"),
        P("wide", "col"),
        P(None, "wide", "col"),
        P(None, "wide", "col"),
        P(None, "col", "wide"),
        P(None, "col", "wide"),
        P(None, "col"),
        P(None, "col"),
    )
    out_specs = (P("wide", "col"), P("wide", None, "col"), P("wide", None, "col"))
    return jax.shard_map(
        per_device, mesh=mesh, in_specs=in_specs, out_specs=out_specs, check_vma=False
    )
```

```python
import jax
import jax.numpy as jnp
from jax import lax
from jax.sharding import PartitionSpec as P

BLK = 128


PRECISE = lax.Precision.HIGHEST


def pick_blocks(source_rows, blocks):
    leading = source_rows.shape[0]
    tiled = source_rows.reshape(leading, source_rows.shape[1] // BLK, BLK)
    selected = jnp.take(tiled, blocks.reshape(-1), axis=1)
    return selected.reshape(leading, blocks.shape[0], blocks.shape[1] * BLK)


def exchange_sum(partial, axis):
    n = lax.axis_size(axis)
    chunk = partial.shape[0] // n
    parts = lax.all_to_all(partial.reshape((n, chunk) + partial.shape[1:]), axis, 0, 0, tiled=False)
    return parts.sum(0)


def exchange_gather(local, axis, dim):
    n = lax.axis_size(axis)
    stacked = jnp.broadcast_to(local[None], (n,) + local.shape)
    parts = lax.all_to_all(stacked, axis, 0, 0, tiled=False)
    parts = jnp.moveaxis(parts, 0, dim)
    return parts.reshape(local.shape[:dim] + (n * local.shape[dim],) + local.shape[dim + 1 :])


def matmul(lhs, rhs, spec):
    return jnp.einsum(spec, lhs, rhs, precision=PRECISE, preferred_element_type=jnp.float32)


def level(z_local, update_partial, inverse):
    update = exchange_sum(update_partial, "col")
    right_side = exchange_gather(z_local - update, "col", 0)
    return exchange_sum(matmul(right_side, inverse, "ski,kij->skj"), "wide")


STREAMS = 2


def stream_rows(z_local, stream):
    rows = z_local.reshape((2, STREAMS, z_local.shape[0] // (2 * STREAMS)) + z_local.shape[1:])[:, stream]
    return rows.reshape((-1,) + z_local.shape[1:])


def one_stream(
    z_root,
    z_child,
    z_grand,
    inv_root,
    inv_child,
    inv_grand,
    panel_child,
    panel_grand,
    anc_child,
    anc_grand,
):
    root_right = exchange_gather(z_root, "col", 0)
    x_root = exchange_sum(matmul(root_right, inv_root, "si,ij->sj"), "wide")
    root_rows = exchange_gather(x_root, "col", 1)
    near_rows = exchange_gather(pick_blocks(root_rows, anc_child), "wide", 0)
    x_child = level(z_child, matmul(near_rows, panel_child, "ska,kaj->skj"), inv_child)
    child_rows = exchange_gather(x_child, "col", 2)
    solved_all = jnp.concatenate([root_rows, child_rows.reshape(child_rows.shape[0], -1)], axis=1)
    far_rows = exchange_gather(pick_blocks(solved_all, anc_grand), "wide", 0)
    x_grand = level(z_grand, matmul(far_rows, panel_grand, "sga,gaj->sgj"), inv_grand)
    return (x_root, x_child, x_grand)


def per_device(z_root, z_child, z_grand, *rest):
    outs = [
        one_stream(stream_rows(z_root, h), stream_rows(z_child, h), stream_rows(z_grand, h), *rest)
        for h in range(STREAMS)
    ]
    return tuple(jnp.concatenate(parts, axis=0) for parts in zip(*outs))


def solution(mesh):
    in_specs = (
        P("col", "wide"),
        P("col", None, "wide"),
        P("col", None, "wide"),
        P("wide", "col"),
        P(None, "wide", "col"),
        P(None, "wide", "col"),
        P(None, "col", "wide"),
        P(None, "col", "wide"),
        P(None, "col"),
        P(None, "col"),
    )
    out_specs = (P("wide", "col"), P("wide", None, "col"), P("wide", None, "col"))
    return jax.shard_map(
        per_device, mesh=mesh, in_specs=in_specs, out_specs=out_specs, check_vma=False
    )
```

```python
import jax
import jax.numpy as jnp
from jax import lax
from jax.sharding import PartitionSpec as P

BLK = 128


PRECISE = lax.Precision.HIGHEST


def pick_blocks(source_rows, blocks):
    leading = source_rows.shape[0]
    tiled = source_rows.reshape(leading, source_rows.shape[1] // BLK, BLK)
    selected = jnp.take(tiled, blocks.reshape(-1), axis=1)
    return selected.reshape(leading, blocks.shape[0], blocks.shape[1] * BLK)


def exchange_sum(partial, axis):
    n = lax.axis_size(axis)
    chunk = partial.shape[0] // n
    parts = lax.all_to_all(partial.reshape((n, chunk) + partial.shape[1:]), axis, 0, 0, tiled=False)
    return parts.sum(0)


def exchange_gather(local, axis, dim):
    n = lax.axis_size(axis)
    stacked = jnp.broadcast_to(local[None], (n,) + local.shape)
    parts = lax.all_to_all(stacked, axis, 0, 0, tiled=False)
    parts = jnp.moveaxis(parts, 0, dim)
    return parts.reshape(local.shape[:dim] + (n * local.shape[dim],) + local.shape[dim + 1 :])


def matmul(lhs, rhs, spec):
    return jnp.einsum(spec, lhs, rhs, precision=PRECISE, preferred_element_type=jnp.float32)


def level(z_local, update_partial, inverse):
    update = exchange_sum(update_partial, "col")
    right_side = exchange_gather(z_local - update, "col", 0)
    return exchange_sum(matmul(right_side, inverse, "ski,kij->skj"), "wide")


def send_blocks(tiles, owner, local):
    here = lax.axis_index("col")
    picked = jnp.take(tiles, local, axis=0)
    outgoing = jnp.where((owner == here)[:, :, None, None], picked, 0.0)
    return lax.all_to_all(outgoing, "col", 0, 0, tiled=False).sum(0)


def slots_of(blocks, per_device):
    rows = blocks.shape[0]
    n_col = blocks.shape[1] // per_device
    return blocks.reshape(rows, n_col, per_device).transpose(1, 0, 2).reshape(n_col, rows * per_device)


def rows_of(received, rows, per_device):
    samples = received.shape[1]
    shaped = received.reshape(rows, per_device, samples, BLK).transpose(2, 0, 1, 3)
    return shaped.reshape(samples, rows, per_device * BLK)


def per_device(
    z_root,
    z_child,
    z_grand,
    inv_root,
    inv_child,
    inv_grand,
    panel_child,
    panel_grand,
    anc_child,
    anc_grand,
):
    n_col = lax.axis_size("col")
    root_right = exchange_gather(z_root, "col", 0)
    x_root = exchange_sum(matmul(root_right, inv_root, "si,ij->sj"), "wide")
    samples, width = x_root.shape
    root_tiles = x_root.reshape(samples, width // BLK, BLK).transpose(1, 0, 2)
    per_root = width // BLK

    child_slots = slots_of(anc_child, anc_child.shape[1] // n_col)
    near_local = send_blocks(root_tiles, child_slots // per_root, child_slots % per_root)
    near_local = rows_of(near_local, anc_child.shape[0], anc_child.shape[1] // n_col)
    near_rows = exchange_gather(near_local, "wide", 0)
    x_child = level(z_child, matmul(near_rows, panel_child, "ska,kaj->skj"), inv_child)

    kids, child_width = x_child.shape[1], x_child.shape[2]
    per_child = child_width // BLK
    child_tiles = x_child.reshape(samples, kids * per_child, BLK).transpose(1, 0, 2)
    all_tiles = jnp.concatenate([root_tiles, child_tiles], axis=0)
    grand_slots = slots_of(anc_grand, anc_grand.shape[1] // n_col)
    root_blocks = per_root * n_col
    is_root = grand_slots < root_blocks
    in_child = grand_slots - root_blocks
    child_block = in_child % (per_child * n_col)
    child_kid = in_child // (per_child * n_col)
    owner = jnp.where(is_root, grand_slots // per_root, child_block // per_child)
    local = jnp.where(is_root, grand_slots % per_root, per_root + child_kid * per_child + child_block % per_child)
    far_local = send_blocks(all_tiles, owner, local)
    far_local = rows_of(far_local, anc_grand.shape[0], anc_grand.shape[1] // n_col)
    far_rows = exchange_gather(far_local, "wide", 0)
    x_grand = level(z_grand, matmul(far_rows, panel_grand, "sga,gaj->sgj"), inv_grand)
    return (x_root, x_child, x_grand)


def solution(mesh):
    in_specs = (
        P("col", "wide"),
        P("col", None, "wide"),
        P("col", None, "wide"),
        P("wide", "col"),
        P(None, "wide", "col"),
        P(None, "wide", "col"),
        P(None, "col", "wide"),
        P(None, "col", "wide"),
        P(None, None),
        P(None, None),
    )
    out_specs = (P("wide", "col"), P("wide", None, "col"), P("wide", None, "col"))
    return jax.shard_map(
        per_device, mesh=mesh, in_specs=in_specs, out_specs=out_specs, check_vma=False
    )
```

```python
import jax
import jax.numpy as jnp
from jax import lax
from jax.sharding import PartitionSpec as P

BLK = 128


PRECISE = lax.Precision.HIGH


def pick_blocks(source_rows, blocks):
    leading = source_rows.shape[0]
    tiled = source_rows.reshape(leading, source_rows.shape[1] // BLK, BLK)
    selected = jnp.take(tiled, blocks.reshape(-1), axis=1)
    return selected.reshape(leading, blocks.shape[0], blocks.shape[1] * BLK)


def exchange_sum(partial, axis):
    n = lax.axis_size(axis)
    chunk = partial.shape[0] // n
    parts = lax.all_to_all(partial.reshape((n, chunk) + partial.shape[1:]), axis, 0, 0, tiled=False)
    return parts.sum(0)


def exchange_gather(local, axis, dim):
    n = lax.axis_size(axis)
    stacked = jnp.broadcast_to(local[None], (n,) + local.shape)
    parts = lax.all_to_all(stacked, axis, 0, 0, tiled=False)
    parts = jnp.moveaxis(parts, 0, dim)
    return parts.reshape(local.shape[:dim] + (n * local.shape[dim],) + local.shape[dim + 1 :])


def matmul(lhs, rhs, spec):
    return jnp.einsum(spec, lhs, rhs, precision=PRECISE, preferred_element_type=jnp.float32)


def level(z_local, update_partial, inverse):
    update = exchange_sum(update_partial, "col")
    right_side = exchange_gather(z_local - update, "col", 0)
    return exchange_sum(matmul(right_side, inverse, "ski,kij->skj"), "wide")


def send_blocks(tiles, owner, local):
    here = lax.axis_index("col")
    picked = jnp.take(tiles, local, axis=0)
    outgoing = jnp.where((owner == here)[:, :, None, None], picked, 0.0)
    return lax.all_to_all(outgoing, "col", 0, 0, tiled=False).sum(0)


def slots_of(blocks, per_device):
    rows = blocks.shape[0]
    n_col = blocks.shape[1] // per_device
    return blocks.reshape(rows, n_col, per_device).transpose(1, 0, 2).reshape(n_col, rows * per_device)


def rows_of(received, rows, per_device):
    samples = received.shape[1]
    shaped = received.reshape(rows, per_device, samples, BLK).transpose(2, 0, 1, 3)
    return shaped.reshape(samples, rows, per_device * BLK)


def per_device(
    z_root,
    z_child,
    z_grand,
    inv_root,
    inv_child,
    inv_grand,
    panel_child,
    panel_grand,
    anc_child,
    anc_grand,
):
    n_col = lax.axis_size("col")
    lists = jnp.concatenate([anc_child.reshape(-1), anc_grand.reshape(-1)]).astype(jnp.float32)
    extra = jnp.zeros((1, z_root.shape[1]), jnp.float32).at[0, : lists.shape[0]].set(lists)
    stacked = exchange_gather(jnp.concatenate([z_root, extra], axis=0)[None], "col", 0)
    root_right = stacked[:, :-1].reshape(-1, z_root.shape[1])
    got = stacked[:, -1, : lists.shape[0]].astype(jnp.int32)
    split = anc_child.size
    anc_child = got[:, :split].reshape((n_col,) + anc_child.shape).transpose(1, 0, 2).reshape(anc_child.shape[0], -1)
    anc_grand = got[:, split:].reshape((n_col,) + anc_grand.shape).transpose(1, 0, 2).reshape(anc_grand.shape[0], -1)
    x_root = exchange_sum(matmul(root_right, inv_root, "si,ij->sj"), "wide")
    samples, width = x_root.shape
    root_tiles = x_root.reshape(samples, width // BLK, BLK).transpose(1, 0, 2)
    per_root = width // BLK

    child_slots = slots_of(anc_child, anc_child.shape[1] // n_col)
    near_local = send_blocks(root_tiles, child_slots // per_root, child_slots % per_root)
    near_local = rows_of(near_local, anc_child.shape[0], anc_child.shape[1] // n_col)
    near_rows = exchange_gather(near_local, "wide", 0)
    x_child = level(z_child, matmul(near_rows, panel_child, "ska,kaj->skj"), inv_child)

    kids, child_width = x_child.shape[1], x_child.shape[2]
    per_child = child_width // BLK
    child_tiles = x_child.reshape(samples, kids * per_child, BLK).transpose(1, 0, 2)
    all_tiles = jnp.concatenate([root_tiles, child_tiles], axis=0)
    grand_slots = slots_of(anc_grand, anc_grand.shape[1] // n_col)
    root_blocks = per_root * n_col
    is_root = grand_slots < root_blocks
    in_child = grand_slots - root_blocks
    child_block = in_child % (per_child * n_col)
    child_kid = in_child // (per_child * n_col)
    owner = jnp.where(is_root, grand_slots // per_root, child_block // per_child)
    local = jnp.where(is_root, grand_slots % per_root, per_root + child_kid * per_child + child_block % per_child)
    far_local = send_blocks(all_tiles, owner, local)
    far_local = rows_of(far_local, anc_grand.shape[0], anc_grand.shape[1] // n_col)
    far_rows = exchange_gather(far_local, "wide", 0)
    x_grand = level(z_grand, matmul(far_rows, panel_grand, "sga,gaj->sgj"), inv_grand)
    return (x_root, x_child, x_grand)


def solution(mesh):
    in_specs = (
        P("col", "wide"),
        P("col", None, "wide"),
        P("col", None, "wide"),
        P("wide", "col"),
        P(None, "wide", "col"),
        P(None, "wide", "col"),
        P(None, "col", "wide"),
        P(None, "col", "wide"),
        P(None, "col"),
        P(None, "col"),
    )
    out_specs = (P("wide", "col"), P("wide", None, "col"), P("wide", None, "col"))
    return jax.shard_map(
        per_device, mesh=mesh, in_specs=in_specs, out_specs=out_specs, check_vma=False
    )
```

```python
import jax
import jax.numpy as jnp
from jax import lax
from jax.sharding import PartitionSpec as P

BLK = 128


PRECISE = lax.Precision.HIGH


def pick_blocks(source_rows, blocks):
    leading = source_rows.shape[0]
    tiled = source_rows.reshape(leading, source_rows.shape[1] // BLK, BLK)
    selected = jnp.take(tiled, blocks.reshape(-1), axis=1)
    return selected.reshape(leading, blocks.shape[0], blocks.shape[1] * BLK)


def exchange_sum(partial, axis):
    n = lax.axis_size(axis)
    chunk = partial.shape[0] // n
    parts = lax.all_to_all(partial.reshape((n, chunk) + partial.shape[1:]), axis, 0, 0, tiled=False)
    return parts.sum(0)


def exchange_gather(local, axis, dim):
    n = lax.axis_size(axis)
    stacked = jnp.broadcast_to(local[None], (n,) + local.shape)
    parts = lax.all_to_all(stacked, axis, 0, 0, tiled=False)
    parts = jnp.moveaxis(parts, 0, dim)
    return parts.reshape(local.shape[:dim] + (n * local.shape[dim],) + local.shape[dim + 1 :])


def matmul(lhs, rhs, spec):
    return jnp.einsum(spec, lhs, rhs, precision=PRECISE, preferred_element_type=jnp.float32)


def level(z_local, update_partial, inverse):
    update = exchange_sum(update_partial, "col")
    right_side = exchange_gather(z_local - update, "col", 0)
    return exchange_sum(matmul(right_side, inverse, "ski,kij->skj"), "wide")


def send_blocks(tiles, mine, local):
    picked = jnp.take(tiles, local, axis=0)
    outgoing = jnp.where(mine[:, :, None, None], picked, 0.0)
    return lax.all_to_all(outgoing, "col", 0, 0, tiled=False).sum(0)


def slots_of(blocks, per_device):
    rows = blocks.shape[0]
    n_col = blocks.shape[1] // per_device
    return blocks.reshape(rows, n_col, per_device).transpose(1, 0, 2).reshape(n_col, rows * per_device)


def rows_of(received, rows, per_device):
    samples = received.shape[1]
    shaped = received.reshape(rows, per_device, samples, BLK).transpose(2, 0, 1, 3)
    return shaped.reshape(samples, rows, per_device * BLK)


def per_device(
    z_root,
    z_child,
    z_grand,
    inv_root,
    inv_child,
    inv_grand,
    panel_child,
    panel_grand,
    anc_child,
    anc_grand,
):
    n_col = lax.axis_size("col")
    lists = jnp.concatenate([anc_child.reshape(-1), anc_grand.reshape(-1)]).astype(jnp.float32)
    extra = jnp.zeros((1, z_root.shape[1]), jnp.float32).at[0, : lists.shape[0]].set(lists)
    here = lax.axis_index("col")
    with_lists, here = lax.optimization_barrier((jnp.concatenate([z_root, extra], axis=0)[None], here))
    stacked = exchange_gather(with_lists, "col", 0)
    root_right = stacked[:, :-1].reshape(-1, z_root.shape[1])
    got = stacked[:, -1, : lists.shape[0]].astype(jnp.int32)
    split = anc_child.size
    anc_child = got[:, :split].reshape((n_col,) + anc_child.shape).transpose(1, 0, 2).reshape(anc_child.shape[0], -1)
    anc_grand = got[:, split:].reshape((n_col,) + anc_grand.shape).transpose(1, 0, 2).reshape(anc_grand.shape[0], -1)
    width = inv_root.shape[1]
    per_root = width // BLK
    kids, child_width = inv_child.shape[0], inv_child.shape[2]
    per_child = child_width // BLK

    child_slots = slots_of(anc_child, anc_child.shape[1] // n_col)
    child_owner, child_local = child_slots // per_root, child_slots % per_root
    grand_slots = slots_of(anc_grand, anc_grand.shape[1] // n_col)
    root_blocks = per_root * n_col
    is_root = grand_slots < root_blocks
    in_child = grand_slots - root_blocks
    child_block = in_child % (per_child * n_col)
    child_kid = in_child // (per_child * n_col)
    owner = jnp.where(is_root, grand_slots // per_root, child_block // per_child)
    local = jnp.where(is_root, grand_slots % per_root, per_root + child_kid * per_child + child_block % per_child)
    child_owner, owner = child_owner == here, owner == here
    root_right, child_owner, child_local, owner, local = lax.optimization_barrier(
        (root_right, child_owner, child_local, owner, local)
    )
    x_root = exchange_sum(matmul(root_right, inv_root, "si,ij->sj"), "wide")
    x_root, child_owner, child_local, owner, local = lax.optimization_barrier(
        (x_root, child_owner, child_local, owner, local)
    )
    root_tiles = x_root.reshape(x_root.shape[0], per_root, BLK).transpose(1, 0, 2)
    near_local = send_blocks(root_tiles, child_owner, child_local)
    near_local = rows_of(near_local, anc_child.shape[0], anc_child.shape[1] // n_col)
    near_rows = exchange_gather(near_local, "wide", 0)
    x_child = level(z_child, matmul(near_rows, panel_child, "ska,kaj->skj"), inv_child)

    x_child, owner, local = lax.optimization_barrier((x_child, owner, local))
    child_tiles = x_child.reshape(x_child.shape[0], kids * per_child, BLK).transpose(1, 0, 2)
    all_tiles = jnp.concatenate([root_tiles, child_tiles], axis=0)
    far_local = send_blocks(all_tiles, owner, local)
    far_local = rows_of(far_local, anc_grand.shape[0], anc_grand.shape[1] // n_col)
    far_rows = exchange_gather(far_local, "wide", 0)
    x_grand = level(z_grand, matmul(far_rows, panel_grand, "sga,gaj->sgj"), inv_grand)
    return (x_root, x_child, x_grand)


def solution(mesh):
    in_specs = (
        P("col", "wide"),
        P("col", None, "wide"),
        P("col", None, "wide"),
        P("wide", "col"),
        P(None, "wide", "col"),
        P(None, "wide", "col"),
        P(None, "col", "wide"),
        P(None, "col", "wide"),
        P(None, "col"),
        P(None, "col"),
    )
    out_specs = (P("wide", "col"), P("wide", None, "col"), P("wide", None, "col"))
    return jax.shard_map(
        per_device, mesh=mesh, in_specs=in_specs, out_specs=out_specs, check_vma=False
    )
```

```python
import jax
import jax.numpy as jnp
from jax import lax
from jax.sharding import PartitionSpec as P

BLK = 128
STREAMS = 2


PRECISE = lax.Precision.HIGH


def exchange_sum(partial, axis):
    n = lax.axis_size(axis)
    chunk = partial.shape[0] // n
    parts = lax.all_to_all(partial.reshape((n, chunk) + partial.shape[1:]), axis, 0, 0, tiled=False)
    return parts.sum(0)


def exchange_gather(local, axis, dim):
    n = lax.axis_size(axis)
    stacked = jnp.broadcast_to(local[None], (n,) + local.shape)
    parts = lax.all_to_all(stacked, axis, 0, 0, tiled=False)
    parts = jnp.moveaxis(parts, 0, dim)
    return parts.reshape(local.shape[:dim] + (n * local.shape[dim],) + local.shape[dim + 1 :])


def shifted(value, axis, step):
    n = lax.axis_size(axis)
    return lax.ppermute(value, axis, [(i, (i + step) % n) for i in range(n)])


def permute_gather(local, axis):
    n = lax.axis_size(axis)
    here = lax.axis_index(axis)
    parts = jnp.stack([local] + [shifted(local, axis, step) for step in range(1, n)])
    ordered = jnp.take(parts, (here - jnp.arange(n)) % n, axis=0)
    return ordered.reshape((n * local.shape[0],) + local.shape[1:])


def permute_sum(chunks, axis):
    n = lax.axis_size(axis)
    here = lax.axis_index(axis)
    total = jnp.take(chunks, here, axis=0)
    for step in range(1, n):
        total = total + shifted(jnp.take(chunks, (here + step) % n, axis=0), axis, step)
    return total


def matmul(lhs, rhs, spec):
    return jnp.einsum(spec, lhs, rhs, precision=PRECISE, preferred_element_type=jnp.float32)


def level(z_local, update_partial, inverse):
    n = lax.axis_size("col")
    update = permute_sum(update_partial.reshape((n, -1) + update_partial.shape[1:]), "col")
    right_side = permute_gather(z_local - update, "col")
    return exchange_sum(matmul(right_side, inverse, "ski,kij->skj"), "wide")


def send_blocks(tiles, mine, local):
    picked = jnp.take(tiles, local, axis=0)
    outgoing = jnp.where(mine[:, :, None, None], picked, 0.0)
    return permute_sum(outgoing, "col")


def slots_of(blocks, per_device):
    rows = blocks.shape[0]
    n_col = blocks.shape[1] // per_device
    return blocks.reshape(rows, n_col, per_device).transpose(1, 0, 2).reshape(n_col, rows * per_device)


def rows_of(received, rows, per_device):
    samples = received.shape[1]
    shaped = received.reshape(rows, per_device, samples, BLK).transpose(2, 0, 1, 3)
    return shaped.reshape(samples, rows, per_device * BLK)


def stream_rows(z_local, stream):
    rows = z_local.reshape((2, STREAMS, z_local.shape[0] // (2 * STREAMS)) + z_local.shape[1:])[:, stream]
    return rows.reshape((-1,) + z_local.shape[1:])


def one_stream(z_root, z_child, z_grand, inv_root, inv_child, inv_grand, panel_child, panel_grand, tables):
    child_mine, child_local, grand_mine, grand_local, child_rows, child_per, grand_rows, grand_per = tables
    root_right = permute_gather(z_root, "col")
    x_root = exchange_sum(matmul(root_right, inv_root, "si,ij->sj"), "wide")
    per_root = x_root.shape[1] // BLK
    root_tiles = x_root.reshape(x_root.shape[0], per_root, BLK).transpose(1, 0, 2)
    near_local = rows_of(send_blocks(root_tiles, child_mine, child_local), child_rows, child_per)
    near_rows = exchange_gather(near_local, "wide", 0)
    x_child = level(z_child, matmul(near_rows, panel_child, "ska,kaj->skj"), inv_child)

    kids, per_child = x_child.shape[1], x_child.shape[2] // BLK
    child_tiles = x_child.reshape(x_child.shape[0], kids * per_child, BLK).transpose(1, 0, 2)
    all_tiles = jnp.concatenate([root_tiles, child_tiles], axis=0)
    far_local = rows_of(send_blocks(all_tiles, grand_mine, grand_local), grand_rows, grand_per)
    far_rows = exchange_gather(far_local, "wide", 0)
    x_grand = level(z_grand, matmul(far_rows, panel_grand, "sga,gaj->sgj"), inv_grand)
    return (x_root, x_child, x_grand)


def per_device(
    z_root,
    z_child,
    z_grand,
    inv_root,
    inv_child,
    inv_grand,
    panel_child,
    panel_grand,
    anc_child,
    anc_grand,
):
    n_col = lax.axis_size("col")
    here = lax.axis_index("col")
    lists = jnp.concatenate([anc_child.reshape(-1), anc_grand.reshape(-1)])
    got = permute_gather(lists[None], "col")
    split = anc_child.size
    anc_child = got[:, :split].reshape((n_col,) + anc_child.shape).transpose(1, 0, 2).reshape(anc_child.shape[0], -1)
    anc_grand = got[:, split:].reshape((n_col,) + anc_grand.shape).transpose(1, 0, 2).reshape(anc_grand.shape[0], -1)

    per_root = inv_root.shape[1] // BLK
    per_child = inv_child.shape[2] // BLK
    child_slots = slots_of(anc_child, anc_child.shape[1] // n_col)
    grand_slots = slots_of(anc_grand, anc_grand.shape[1] // n_col)
    root_blocks = per_root * n_col
    is_root = grand_slots < root_blocks
    in_child = grand_slots - root_blocks
    child_block = in_child % (per_child * n_col)
    child_kid = in_child // (per_child * n_col)
    owner = jnp.where(is_root, grand_slots // per_root, child_block // per_child)
    local = jnp.where(is_root, grand_slots % per_root, per_root + child_kid * per_child + child_block % per_child)
    tables = (
        child_slots // per_root == here,
        child_slots % per_root,
        owner == here,
        local,
        anc_child.shape[0],
        anc_child.shape[1] // n_col,
        anc_grand.shape[0],
        anc_grand.shape[1] // n_col,
    )
    outs = [
        one_stream(
            stream_rows(z_root, h),
            stream_rows(z_child, h),
            stream_rows(z_grand, h),
            inv_root,
            inv_child,
            inv_grand,
            panel_child,
            panel_grand,
            tables,
        )
        for h in range(STREAMS)
    ]
    return tuple(jnp.concatenate(parts, axis=0) for parts in zip(*outs))


def solution(mesh):
    in_specs = (
        P("col", "wide"),
        P("col", None, "wide"),
        P("col", None, "wide"),
        P("wide", "col"),
        P(None, "wide", "col"),
        P(None, "wide", "col"),
        P(None, "col", "wide"),
        P(None, "col", "wide"),
        P(None, "col"),
        P(None, "col"),
    )
    out_specs = (P("wide", "col"), P("wide", None, "col"), P("wide", None, "col"))
    return jax.shard_map(
        per_device, mesh=mesh, in_specs=in_specs, out_specs=out_specs, check_vma=False
    )
```

```python
import jax
import jax.numpy as jnp
from jax import lax
from jax.sharding import PartitionSpec as P

BLK = 128


PRECISE = lax.Precision.HIGH


def pick_blocks(source_rows, blocks):
    leading = source_rows.shape[0]
    tiled = source_rows.reshape(leading, source_rows.shape[1] // BLK, BLK)
    selected = jnp.take(tiled, blocks.reshape(-1), axis=1)
    return selected.reshape(leading, blocks.shape[0], blocks.shape[1] * BLK)


def exchange_sum(partial, axis):
    n = lax.axis_size(axis)
    chunk = partial.shape[0] // n
    parts = lax.all_to_all(partial.reshape((n, chunk) + partial.shape[1:]), axis, 0, 0, tiled=False)
    return parts.sum(0)


def exchange_gather(local, axis, dim):
    n = lax.axis_size(axis)
    stacked = jnp.broadcast_to(local[None], (n,) + local.shape)
    parts = lax.all_to_all(stacked, axis, 0, 0, tiled=False)
    parts = jnp.moveaxis(parts, 0, dim)
    return parts.reshape(local.shape[:dim] + (n * local.shape[dim],) + local.shape[dim + 1 :])


def chip_groups(n):
    return [[2 * x + core for x in range(n // 2)] for core in range(2)]


def col_sum(chunks, cores):
    n = lax.axis_size("col")
    paired = chunks.reshape((n // 2, 2) + chunks.shape[1:])
    mine = lax.dynamic_index_in_dim(paired, cores[0], axis=1, keepdims=False)
    other = lax.dynamic_index_in_dim(paired, cores[1], axis=1, keepdims=False)
    chip = mine + lax.ppermute(other, "col", [(d, d ^ 1) for d in range(n)])
    parts = lax.all_to_all(chip, "col", 0, 0, tiled=False, axis_index_groups=chip_groups(n))
    return parts.sum(0)


def col_gather(local, cores):
    n = lax.axis_size("col")
    stacked = jnp.broadcast_to(local[None], (n // 2,) + local.shape)
    same = lax.all_to_all(stacked, "col", 0, 0, tiled=False, axis_index_groups=chip_groups(n))
    other = lax.ppermute(same, "col", [(d, d ^ 1) for d in range(n)])
    both = jnp.where(cores[2], jnp.stack([same, other], 1), jnp.stack([other, same], 1))
    return both.reshape((n,) + local.shape)


def matmul(lhs, rhs, spec):
    return jnp.einsum(spec, lhs, rhs, precision=PRECISE, preferred_element_type=jnp.float32)


def level(z_local, update_partial, inverse, cores):
    n = lax.axis_size("col")
    update = col_sum(update_partial.reshape((n, -1) + update_partial.shape[1:]), cores)
    right_side = col_gather(z_local - update, cores)
    right_side = right_side.reshape((-1,) + right_side.shape[2:])
    return exchange_sum(matmul(right_side, inverse, "ski,kij->skj"), "wide")


def send_blocks(tiles, mine, local, cores):
    picked = jnp.take(tiles, local, axis=0)
    outgoing = jnp.where(mine[:, :, None, None], picked, 0.0)
    return col_sum(outgoing, cores)


def slots_of(blocks, per_device):
    rows = blocks.shape[0]
    n_col = blocks.shape[1] // per_device
    return blocks.reshape(rows, n_col, per_device).transpose(1, 0, 2).reshape(n_col, rows * per_device)


def rows_of(received, rows, per_device):
    samples = received.shape[1]
    shaped = received.reshape(rows, per_device, samples, BLK).transpose(2, 0, 1, 3)
    return shaped.reshape(samples, rows, per_device * BLK)


def per_device(
    z_root,
    z_child,
    z_grand,
    inv_root,
    inv_child,
    inv_grand,
    panel_child,
    panel_grand,
    anc_child,
    anc_grand,
):
    n_col = lax.axis_size("col")
    lists = jnp.concatenate([anc_child.reshape(-1), anc_grand.reshape(-1)]).astype(jnp.float32)
    extra = jnp.zeros((1, z_root.shape[1]), jnp.float32).at[0, : lists.shape[0]].set(lists)
    here = lax.axis_index("col")
    cores = (here % 2, 1 - here % 2, here % 2 == 0)
    with_lists, here, cores = lax.optimization_barrier((jnp.concatenate([z_root, extra], axis=0)[None], here, cores))
    stacked = col_gather(with_lists[0], cores)
    root_right = stacked[:, :-1].reshape(-1, z_root.shape[1])
    got = stacked[:, -1, : lists.shape[0]].astype(jnp.int32)
    split = anc_child.size
    anc_child = got[:, :split].reshape((n_col,) + anc_child.shape).transpose(1, 0, 2).reshape(anc_child.shape[0], -1)
    anc_grand = got[:, split:].reshape((n_col,) + anc_grand.shape).transpose(1, 0, 2).reshape(anc_grand.shape[0], -1)
    width = inv_root.shape[1]
    per_root = width // BLK
    kids, child_width = inv_child.shape[0], inv_child.shape[2]
    per_child = child_width // BLK

    child_slots = slots_of(anc_child, anc_child.shape[1] // n_col)
    child_owner, child_local = child_slots // per_root, child_slots % per_root
    grand_slots = slots_of(anc_grand, anc_grand.shape[1] // n_col)
    root_blocks = per_root * n_col
    is_root = grand_slots < root_blocks
    in_child = grand_slots - root_blocks
    child_block = in_child % (per_child * n_col)
    child_kid = in_child // (per_child * n_col)
    owner = jnp.where(is_root, grand_slots // per_root, child_block // per_child)
    local = jnp.where(is_root, grand_slots % per_root, per_root + child_kid * per_child + child_block % per_child)
    child_owner, owner = child_owner == here, owner == here
    root_right, child_owner, child_local, owner, local, cores = lax.optimization_barrier(
        (root_right, child_owner, child_local, owner, local, cores)
    )
    x_root = exchange_sum(matmul(root_right, inv_root, "si,ij->sj"), "wide")
    x_root, child_owner, child_local, owner, local, cores = lax.optimization_barrier(
        (x_root, child_owner, child_local, owner, local, cores)
    )
    root_tiles = x_root.reshape(x_root.shape[0], per_root, BLK).transpose(1, 0, 2)
    near_local = send_blocks(root_tiles, child_owner, child_local, cores)
    near_local = rows_of(near_local, anc_child.shape[0], anc_child.shape[1] // n_col)
    near_rows = exchange_gather(near_local, "wide", 0)
    x_child = level(z_child, matmul(near_rows, panel_child, "ska,kaj->skj"), inv_child, cores)

    x_child, owner, local, cores = lax.optimization_barrier((x_child, owner, local, cores))
    child_tiles = x_child.reshape(x_child.shape[0], kids * per_child, BLK).transpose(1, 0, 2)
    all_tiles = jnp.concatenate([root_tiles, child_tiles], axis=0)
    far_local = send_blocks(all_tiles, owner, local, cores)
    far_local = rows_of(far_local, anc_grand.shape[0], anc_grand.shape[1] // n_col)
    far_rows = exchange_gather(far_local, "wide", 0)
    x_grand = level(z_grand, matmul(far_rows, panel_grand, "sga,gaj->sgj"), inv_grand, cores)
    return (x_root, x_child, x_grand)


def solution(mesh):
    in_specs = (
        P("col", "wide"),
        P("col", None, "wide"),
        P("col", None, "wide"),
        P("wide", "col"),
        P(None, "wide", "col"),
        P(None, "wide", "col"),
        P(None, "col", "wide"),
        P(None, "col", "wide"),
        P(None, "col"),
        P(None, "col"),
    )
    out_specs = (P("wide", "col"), P("wide", None, "col"), P("wide", None, "col"))
    return jax.shard_map(
        per_device, mesh=mesh, in_specs=in_specs, out_specs=out_specs, check_vma=False
    )
```

```python
import jax
import jax.numpy as jnp
from jax import lax
from jax.sharding import PartitionSpec as P

BLK = 128


PRECISE = lax.Precision.HIGH


def pick_blocks(source_rows, blocks):
    leading = source_rows.shape[0]
    tiled = source_rows.reshape(leading, source_rows.shape[1] // BLK, BLK)
    selected = jnp.take(tiled, blocks.reshape(-1), axis=1)
    return selected.reshape(leading, blocks.shape[0], blocks.shape[1] * BLK)


def exchange_sum(partial, axis):
    n = lax.axis_size(axis)
    chunk = partial.shape[0] // n
    parts = lax.all_to_all(partial.reshape((n, chunk) + partial.shape[1:]), axis, 0, 0, tiled=False)
    return parts.sum(0)


def exchange_gather(local, axis, dim):
    n = lax.axis_size(axis)
    stacked = jnp.broadcast_to(local[None], (n,) + local.shape)
    parts = lax.all_to_all(stacked, axis, 0, 0, tiled=False)
    parts = jnp.moveaxis(parts, 0, dim)
    return parts.reshape(local.shape[:dim] + (n * local.shape[dim],) + local.shape[dim + 1 :])


def chip_groups(n):
    return [[2 * x + core for x in range(n // 2)] for core in range(2)]


def col_sum(chunks, cores):
    n = lax.axis_size("col")
    paired = chunks.reshape((n // 2, 2) + chunks.shape[1:])
    mine = lax.dynamic_index_in_dim(paired, cores[0], axis=1, keepdims=False)
    other = lax.dynamic_index_in_dim(paired, cores[1], axis=1, keepdims=False)
    chip = mine + lax.ppermute(other, "col", [(d, d ^ 1) for d in range(n)])
    parts = lax.all_to_all(chip, "col", 0, 0, tiled=False, axis_index_groups=chip_groups(n))
    return parts.sum(0)


def col_gather(local, cores):
    n = lax.axis_size("col")
    stacked = jnp.broadcast_to(local[None], (n // 2,) + local.shape)
    same = lax.all_to_all(stacked, "col", 0, 0, tiled=False, axis_index_groups=chip_groups(n))
    other = lax.ppermute(same, "col", [(d, d ^ 1) for d in range(n)])
    both = jnp.where(cores[2], jnp.stack([same, other], 1), jnp.stack([other, same], 1))
    return both.reshape((n,) + local.shape)


def matmul(lhs, rhs, spec):
    return jnp.einsum(spec, lhs, rhs, precision=PRECISE, preferred_element_type=jnp.float32)


def level(z_local, near_rows, panel, spec, inverse, cores):
    n = lax.axis_size("col")
    paired = near_rows.reshape((n // 2, 2, -1) + near_rows.shape[1:])
    other = lax.dynamic_index_in_dim(paired, cores[1], axis=1, keepdims=False)
    other = matmul(other.reshape((-1,) + other.shape[2:]), panel, spec)
    sent = lax.ppermute(other.reshape((n // 2, -1) + other.shape[1:]), "col", [(d, d ^ 1) for d in range(n)])
    mine = lax.dynamic_index_in_dim(paired, cores[0], axis=1, keepdims=False)
    mine = matmul(mine.reshape((-1,) + mine.shape[2:]), panel, spec)
    chip = mine.reshape(sent.shape) + sent
    update = lax.all_to_all(chip, "col", 0, 0, tiled=False, axis_index_groups=chip_groups(n)).sum(0)
    right_side = col_gather(z_local - update, cores)
    right_side = right_side.reshape((-1,) + right_side.shape[2:])
    return exchange_sum(matmul(right_side, inverse, "ski,kij->skj"), "wide")


def send_blocks(tiles, mine, local, cores):
    picked = jnp.take(tiles, local, axis=0)
    outgoing = jnp.where(mine[:, :, None, None], picked, 0.0)
    return col_sum(outgoing, cores)


def slots_of(blocks, per_device):
    rows = blocks.shape[0]
    n_col = blocks.shape[1] // per_device
    return blocks.reshape(rows, n_col, per_device).transpose(1, 0, 2).reshape(n_col, rows * per_device)


def rows_of(received, rows, per_device):
    samples = received.shape[1]
    shaped = received.reshape(rows, per_device, samples, BLK).transpose(2, 0, 1, 3)
    return shaped.reshape(samples, rows, per_device * BLK)


def per_device(
    z_root,
    z_child,
    z_grand,
    inv_root,
    inv_child,
    inv_grand,
    panel_child,
    panel_grand,
    anc_child,
    anc_grand,
):
    n_col = lax.axis_size("col")
    lists = jnp.concatenate([anc_child.reshape(-1), anc_grand.reshape(-1)]).astype(jnp.float32)
    extra = jnp.zeros((1, z_root.shape[1]), jnp.float32).at[0, : lists.shape[0]].set(lists)
    here = lax.axis_index("col")
    cores = (here % 2, 1 - here % 2, here % 2 == 0)
    with_lists, here, cores = lax.optimization_barrier((jnp.concatenate([z_root, extra], axis=0)[None], here, cores))
    stacked = col_gather(with_lists[0], cores)
    root_right = stacked[:, :-1].reshape(-1, z_root.shape[1])
    got = stacked[:, -1, : lists.shape[0]].astype(jnp.int32)
    split = anc_child.size
    anc_child = got[:, :split].reshape((n_col,) + anc_child.shape).transpose(1, 0, 2).reshape(anc_child.shape[0], -1)
    anc_grand = got[:, split:].reshape((n_col,) + anc_grand.shape).transpose(1, 0, 2).reshape(anc_grand.shape[0], -1)
    width = inv_root.shape[1]
    per_root = width // BLK
    kids, child_width = inv_child.shape[0], inv_child.shape[2]
    per_child = child_width // BLK

    child_slots = slots_of(anc_child, anc_child.shape[1] // n_col)
    child_owner, child_local = child_slots // per_root, child_slots % per_root
    grand_slots = slots_of(anc_grand, anc_grand.shape[1] // n_col)
    root_blocks = per_root * n_col
    is_root = grand_slots < root_blocks
    in_child = grand_slots - root_blocks
    child_block = in_child % (per_child * n_col)
    child_kid = in_child // (per_child * n_col)
    owner = jnp.where(is_root, grand_slots // per_root, child_block // per_child)
    local = jnp.where(is_root, grand_slots % per_root, per_root + child_kid * per_child + child_block % per_child)
    child_owner, owner = child_owner == here, owner == here
    root_right, child_owner, child_local, owner, local, cores = lax.optimization_barrier(
        (root_right, child_owner, child_local, owner, local, cores)
    )
    x_root = exchange_sum(matmul(root_right, inv_root, "si,ij->sj"), "wide")
    x_root, child_owner, child_local, owner, local, cores = lax.optimization_barrier(
        (x_root, child_owner, child_local, owner, local, cores)
    )
    root_tiles = x_root.reshape(x_root.shape[0], per_root, BLK).transpose(1, 0, 2)
    near_local = send_blocks(root_tiles, child_owner, child_local, cores)
    near_local = rows_of(near_local, anc_child.shape[0], anc_child.shape[1] // n_col)
    near_rows = exchange_gather(near_local, "wide", 0)
    x_child = level(z_child, near_rows, panel_child, "ska,kaj->skj", inv_child, cores)

    x_child, owner, local, cores = lax.optimization_barrier((x_child, owner, local, cores))
    child_tiles = x_child.reshape(x_child.shape[0], kids * per_child, BLK).transpose(1, 0, 2)
    all_tiles = jnp.concatenate([root_tiles, child_tiles], axis=0)
    far_local = send_blocks(all_tiles, owner, local, cores)
    far_local = rows_of(far_local, anc_grand.shape[0], anc_grand.shape[1] // n_col)
    far_rows = exchange_gather(far_local, "wide", 0)
    x_grand = level(z_grand, far_rows, panel_grand, "sga,gaj->sgj", inv_grand, cores)
    return (x_root, x_child, x_grand)


def solution(mesh):
    in_specs = (
        P("col", "wide"),
        P("col", None, "wide"),
        P("col", None, "wide"),
        P("wide", "col"),
        P(None, "wide", "col"),
        P(None, "wide", "col"),
        P(None, "col", "wide"),
        P(None, "col", "wide"),
        P(None, "col"),
        P(None, "col"),
    )
    out_specs = (P("wide", "col"), P("wide", None, "col"), P("wide", None, "col"))
    return jax.shard_map(
        per_device, mesh=mesh, in_specs=in_specs, out_specs=out_specs, check_vma=False
    )
```

```python
import jax
import jax.numpy as jnp
from jax import lax
from jax.sharding import PartitionSpec as P

BLK = 128


PRECISE = lax.Precision.HIGH


def pick_blocks(source_rows, blocks):
    leading = source_rows.shape[0]
    tiled = source_rows.reshape(leading, source_rows.shape[1] // BLK, BLK)
    selected = jnp.take(tiled, blocks.reshape(-1), axis=1)
    return selected.reshape(leading, blocks.shape[0], blocks.shape[1] * BLK)


def exchange_sum(partial, axis):
    n = lax.axis_size(axis)
    chunk = partial.shape[0] // n
    parts = lax.all_to_all(partial.reshape((n, chunk) + partial.shape[1:]), axis, 0, 0, tiled=False)
    return parts.sum(0)


def exchange_gather(local, axis, dim):
    n = lax.axis_size(axis)
    stacked = jnp.broadcast_to(local[None], (n,) + local.shape)
    parts = lax.all_to_all(stacked, axis, 0, 0, tiled=False)
    parts = jnp.moveaxis(parts, 0, dim)
    return parts.reshape(local.shape[:dim] + (n * local.shape[dim],) + local.shape[dim + 1 :])


def chip_groups(n):
    return [[2 * x + core for x in range(n // 2)] for core in range(2)]


def pick_core(paired, index):
    taken = lax.dynamic_slice_in_dim(paired, index, 1, axis=1, allow_negative_indices=False)
    return taken.reshape(paired.shape[:1] + paired.shape[2:])


def col_sum(chunks, cores):
    n = lax.axis_size("col")
    paired = chunks.reshape((n // 2, 2) + chunks.shape[1:])
    mine = pick_core(paired, cores[0])
    other = pick_core(paired, cores[1])
    chip = mine + lax.ppermute(other, "col", [(d, d ^ 1) for d in range(n)])
    parts = lax.all_to_all(chip, "col", 0, 0, tiled=False, axis_index_groups=chip_groups(n))
    return parts.sum(0)


def col_gather(local, cores):
    n = lax.axis_size("col")
    stacked = jnp.broadcast_to(local[None], (n // 2,) + local.shape)
    same = lax.all_to_all(stacked, "col", 0, 0, tiled=False, axis_index_groups=chip_groups(n))
    other = lax.ppermute(same, "col", [(d, d ^ 1) for d in range(n)])
    both = jnp.where(cores[2], jnp.stack([same, other], 1), jnp.stack([other, same], 1))
    return both.reshape((n,) + local.shape)


def matmul(lhs, rhs, spec):
    return jnp.einsum(spec, lhs, rhs, precision=PRECISE, preferred_element_type=jnp.float32)


def level(z_local, update_partial, inverse, cores):
    n = lax.axis_size("col")
    update = col_sum(update_partial.reshape((n, -1) + update_partial.shape[1:]), cores)
    right_side = col_gather(z_local - update, cores)
    right_side = right_side.reshape((-1,) + right_side.shape[2:])
    return exchange_sum(matmul(right_side, inverse, "ski,kij->skj"), "wide")


def send_blocks(tiles, tables):
    other_mine, other_local, own_mine, own_local = tables
    n = 2 * other_mine.shape[0]
    other = jnp.where(other_mine[:, :, None, None], jnp.take(tiles, other_local, axis=0), 0.0)
    sent = lax.ppermute(other, "col", [(d, d ^ 1) for d in range(n)])
    own = jnp.where(own_mine[:, :, None, None], jnp.take(tiles, own_local, axis=0), 0.0)
    parts = lax.all_to_all(own + sent, "col", 0, 0, tiled=False, axis_index_groups=chip_groups(n))
    return parts.sum(0)


def by_core(table, cores):
    paired = table.reshape((table.shape[0] // 2, 2) + table.shape[1:])
    return (
        pick_core(paired, cores[1]),
        pick_core(paired, cores[0]),
    )


def slots_of(blocks, per_device):
    rows = blocks.shape[0]
    n_col = blocks.shape[1] // per_device
    return blocks.reshape(rows, n_col, per_device).transpose(1, 0, 2).reshape(n_col, rows * per_device)


def rows_of(received, rows, per_device):
    samples = received.shape[1]
    shaped = received.reshape(rows, per_device, samples, BLK).transpose(2, 0, 1, 3)
    return shaped.reshape(samples, rows, per_device * BLK)


def per_device(
    z_root,
    z_child,
    z_grand,
    inv_root,
    inv_child,
    inv_grand,
    panel_child,
    panel_grand,
    anc_child,
    anc_grand,
):
    n_col = lax.axis_size("col")
    lists = jnp.concatenate([anc_child.reshape(-1), anc_grand.reshape(-1)]).astype(jnp.float32)
    extra = jnp.zeros((1, z_root.shape[1]), jnp.float32).at[0, : lists.shape[0]].set(lists)
    here = lax.axis_index("col")
    cores = (here % 2, 1 - here % 2, here % 2 == 0)
    with_lists, here, cores = lax.optimization_barrier((jnp.concatenate([z_root, extra], axis=0)[None], here, cores))
    stacked = col_gather(with_lists[0], cores)
    root_right = stacked[:, :-1].reshape(-1, z_root.shape[1])
    got = stacked[:, -1, : lists.shape[0]].astype(jnp.int32)
    split = anc_child.size
    anc_child = got[:, :split].reshape((n_col,) + anc_child.shape).transpose(1, 0, 2).reshape(anc_child.shape[0], -1)
    anc_grand = got[:, split:].reshape((n_col,) + anc_grand.shape).transpose(1, 0, 2).reshape(anc_grand.shape[0], -1)
    width = inv_root.shape[1]
    per_root = width // BLK
    kids, child_width = inv_child.shape[0], inv_child.shape[2]
    per_child = child_width // BLK

    child_slots = slots_of(anc_child, anc_child.shape[1] // n_col)
    child_owner, child_local = child_slots // per_root, child_slots % per_root
    grand_slots = slots_of(anc_grand, anc_grand.shape[1] // n_col)
    root_blocks = per_root * n_col
    is_root = grand_slots < root_blocks
    in_child = grand_slots - root_blocks
    child_block = in_child % (per_child * n_col)
    child_kid = in_child // (per_child * n_col)
    owner = jnp.where(is_root, grand_slots // per_root, child_block // per_child)
    local = jnp.where(is_root, grand_slots % per_root, per_root + child_kid * per_child + child_block % per_child)
    child_owner, owner = child_owner == here, owner == here
    child_tables = by_core(child_owner, cores) + by_core(child_local, cores)
    child_tables = (child_tables[0], child_tables[2], child_tables[1], child_tables[3])
    grand_tables = by_core(owner, cores) + by_core(local, cores)
    grand_tables = (grand_tables[0], grand_tables[2], grand_tables[1], grand_tables[3])
    root_right, child_tables, grand_tables, cores = lax.optimization_barrier(
        (root_right, child_tables, grand_tables, cores)
    )
    x_root = exchange_sum(matmul(root_right, inv_root, "si,ij->sj"), "wide")
    x_root, child_tables, grand_tables, cores = lax.optimization_barrier(
        (x_root, child_tables, grand_tables, cores)
    )
    root_tiles = x_root.reshape(x_root.shape[0], per_root, BLK).transpose(1, 0, 2)
    near_local = send_blocks(root_tiles, child_tables)
    near_local = rows_of(near_local, anc_child.shape[0], anc_child.shape[1] // n_col)
    near_rows = exchange_gather(near_local, "wide", 0)
    x_child = level(z_child, matmul(near_rows, panel_child, "ska,kaj->skj"), inv_child, cores)

    x_child, grand_tables, cores = lax.optimization_barrier((x_child, grand_tables, cores))
    child_tiles = x_child.reshape(x_child.shape[0], kids * per_child, BLK).transpose(1, 0, 2)
    all_tiles = jnp.concatenate([root_tiles, child_tiles], axis=0)
    far_local = send_blocks(all_tiles, grand_tables)
    far_local = rows_of(far_local, anc_grand.shape[0], anc_grand.shape[1] // n_col)
    far_rows = exchange_gather(far_local, "wide", 0)
    x_grand = level(z_grand, matmul(far_rows, panel_grand, "sga,gaj->sgj"), inv_grand, cores)
    return (x_root, x_child, x_grand)


def solution(mesh):
    in_specs = (
        P("col", "wide"),
        P("col", None, "wide"),
        P("col", None, "wide"),
        P("wide", "col"),
        P(None, "wide", "col"),
        P(None, "wide", "col"),
        P(None, "col", "wide"),
        P(None, "col", "wide"),
        P(None, "col"),
        P(None, "col"),
    )
    out_specs = (P("wide", "col"), P("wide", None, "col"), P("wide", None, "col"))
    return jax.shard_map(
        per_device, mesh=mesh, in_specs=in_specs, out_specs=out_specs, check_vma=False
    )
```

```python
import jax
import jax.numpy as jnp
from jax import lax
from jax.sharding import PartitionSpec as P

BLK = 128


PRECISE = lax.Precision.HIGH


def pick_blocks(source_rows, blocks):
    leading = source_rows.shape[0]
    tiled = source_rows.reshape(leading, source_rows.shape[1] // BLK, BLK)
    selected = jnp.take(tiled, blocks.reshape(-1), axis=1)
    return selected.reshape(leading, blocks.shape[0], blocks.shape[1] * BLK)


def exchange_sum(partial, axis):
    n = lax.axis_size(axis)
    chunk = partial.shape[0] // n
    parts = lax.all_to_all(partial.reshape((n, chunk) + partial.shape[1:]), axis, 0, 0, tiled=False)
    return parts.sum(0)


def exchange_gather(local, axis, dim):
    n = lax.axis_size(axis)
    stacked = jnp.broadcast_to(local[None], (n,) + local.shape)
    parts = lax.all_to_all(stacked, axis, 0, 0, tiled=False)
    parts = jnp.moveaxis(parts, 0, dim)
    return parts.reshape(local.shape[:dim] + (n * local.shape[dim],) + local.shape[dim + 1 :])


def chip_groups(n):
    return [[2 * x + core for x in range(n // 2)] for core in range(2)]


def pick_core(paired, index):
    taken = lax.dynamic_slice_in_dim(paired, index, 1, axis=1, allow_negative_indices=False)
    return taken.reshape(paired.shape[:1] + paired.shape[2:])


def col_sum(chunks, cores):
    n = lax.axis_size("col")
    paired = chunks.reshape((n // 2, 2) + chunks.shape[1:])
    mine = pick_core(paired, cores[0])
    other = pick_core(paired, cores[1])
    chip = mine + lax.ppermute(other, "col", [(d, d ^ 1) for d in range(n)])
    parts = lax.all_to_all(chip, "col", 0, 0, tiled=False, axis_index_groups=chip_groups(n))
    return parts.sum(0)


def col_halves(local):
    n = lax.axis_size("col")
    stacked = jnp.broadcast_to(local[None], (n // 2,) + local.shape)
    same = lax.all_to_all(stacked, "col", 0, 0, tiled=False, axis_index_groups=chip_groups(n))
    other = lax.ppermute(same, "col", [(d, d ^ 1) for d in range(n)])
    return same, other


def col_join(same, other, cores):
    both = jnp.where(cores[2], jnp.stack([same, other], 1), jnp.stack([other, same], 1))
    return both.reshape((-1,) + same.shape[1:])


def col_gather(local, cores):
    return col_join(*col_halves(local), cores)


def matmul(lhs, rhs, spec):
    return jnp.einsum(spec, lhs, rhs, precision=PRECISE, preferred_element_type=jnp.float32)


def level(z_local, update_partial, inverse, cores):
    n = lax.axis_size("col")
    update = col_sum(update_partial.reshape((n, -1) + update_partial.shape[1:]), cores)
    right_side = col_gather(z_local - update, cores)
    right_side = right_side.reshape((-1,) + right_side.shape[2:])
    return exchange_sum(matmul(right_side, inverse, "ski,kij->skj"), "wide")


def send_blocks(tiles, tables):
    other_mine, other_local, own_mine, own_local = tables
    n = 2 * other_mine.shape[0]
    other = jnp.where(other_mine[:, :, None, None], jnp.take(tiles, other_local, axis=0), 0.0)
    sent = lax.ppermute(other, "col", [(d, d ^ 1) for d in range(n)])
    own = jnp.where(own_mine[:, :, None, None], jnp.take(tiles, own_local, axis=0), 0.0)
    parts = lax.all_to_all(own + sent, "col", 0, 0, tiled=False, axis_index_groups=chip_groups(n))
    return parts.sum(0)


def by_core(table, cores):
    paired = table.reshape((table.shape[0] // 2, 2) + table.shape[1:])
    return (
        pick_core(paired, cores[1]),
        pick_core(paired, cores[0]),
    )


def slots_of(blocks, per_device):
    rows = blocks.shape[0]
    n_col = blocks.shape[1] // per_device
    return blocks.reshape(rows, n_col, per_device).transpose(1, 0, 2).reshape(n_col, rows * per_device)


def rows_of(received, rows, per_device):
    samples = received.shape[1]
    shaped = received.reshape(rows, per_device, samples, BLK).transpose(2, 0, 1, 3)
    return shaped.reshape(samples, rows, per_device * BLK)


def per_device(
    z_root,
    z_child,
    z_grand,
    inv_root,
    inv_child,
    inv_grand,
    panel_child,
    panel_grand,
    anc_child,
    anc_grand,
):
    n_col = lax.axis_size("col")
    lists = jnp.concatenate([anc_child.reshape(-1), anc_grand.reshape(-1)]).astype(jnp.float32)
    extra = jnp.zeros((8, z_root.shape[1]), jnp.float32).at[0, : lists.shape[0]].set(lists)
    here = lax.axis_index("col")
    cores = (here % 2, 1 - here % 2, here % 2 == 0)
    with_lists, here, cores = lax.optimization_barrier((jnp.concatenate([z_root, extra], axis=0)[None], here, cores))
    same, other = col_halves(with_lists[0])
    rows = z_root.shape[0]
    root_right = col_join(same[:, :rows], other[:, :rows], cores).reshape(-1, z_root.shape[1])
    got = col_join(same[:, rows : rows + 1], other[:, rows : rows + 1], cores)[:, 0, : lists.shape[0]].astype(jnp.int32)
    split = anc_child.size
    anc_child = got[:, :split].reshape((n_col,) + anc_child.shape).transpose(1, 0, 2).reshape(anc_child.shape[0], -1)
    anc_grand = got[:, split:].reshape((n_col,) + anc_grand.shape).transpose(1, 0, 2).reshape(anc_grand.shape[0], -1)
    width = inv_root.shape[1]
    per_root = width // BLK
    kids, child_width = inv_child.shape[0], inv_child.shape[2]
    per_child = child_width // BLK

    child_slots = slots_of(anc_child, anc_child.shape[1] // n_col)
    child_owner, child_local = child_slots // per_root, child_slots % per_root
    grand_slots = slots_of(anc_grand, anc_grand.shape[1] // n_col)
    root_blocks = per_root * n_col
    is_root = grand_slots < root_blocks
    in_child = grand_slots - root_blocks
    child_block = in_child % (per_child * n_col)
    child_kid = in_child // (per_child * n_col)
    owner = jnp.where(is_root, grand_slots // per_root, child_block // per_child)
    local = jnp.where(is_root, grand_slots % per_root, per_root + child_kid * per_child + child_block % per_child)
    child_owner, owner = child_owner == here, owner == here
    child_tables = by_core(child_owner, cores) + by_core(child_local, cores)
    child_tables = (child_tables[0], child_tables[2], child_tables[1], child_tables[3])
    grand_tables = by_core(owner, cores) + by_core(local, cores)
    grand_tables = (grand_tables[0], grand_tables[2], grand_tables[1], grand_tables[3])
    root_right, child_tables, grand_tables, cores = lax.optimization_barrier(
        (root_right, child_tables, grand_tables, cores)
    )
    x_root = exchange_sum(matmul(root_right, inv_root, "si,ij->sj"), "wide")
    x_root, child_tables, grand_tables, cores = lax.optimization_barrier(
        (x_root, child_tables, grand_tables, cores)
    )
    root_tiles = x_root.reshape(x_root.shape[0], per_root, BLK).transpose(1, 0, 2)
    near_local = send_blocks(root_tiles, child_tables)
    near_local = rows_of(near_local, anc_child.shape[0], anc_child.shape[1] // n_col)
    near_rows = exchange_gather(near_local, "wide", 0)
    x_child = level(z_child, matmul(near_rows, panel_child, "ska,kaj->skj"), inv_child, cores)

    x_child, grand_tables, cores = lax.optimization_barrier((x_child, grand_tables, cores))
    child_tiles = x_child.reshape(x_child.shape[0], kids * per_child, BLK).transpose(1, 0, 2)
    all_tiles = jnp.concatenate([root_tiles, child_tiles], axis=0)
    far_local = send_blocks(all_tiles, grand_tables)
    far_local = rows_of(far_local, anc_grand.shape[0], anc_grand.shape[1] // n_col)
    far_rows = exchange_gather(far_local, "wide", 0)
    x_grand = level(z_grand, matmul(far_rows, panel_grand, "sga,gaj->sgj"), inv_grand, cores)
    return (x_root, x_child, x_grand)


def solution(mesh):
    in_specs = (
        P("col", "wide"),
        P("col", None, "wide"),
        P("col", None, "wide"),
        P("wide", "col"),
        P(None, "wide", "col"),
        P(None, "wide", "col"),
        P(None, "col", "wide"),
        P(None, "col", "wide"),
        P(None, "col"),
        P(None, "col"),
    )
    out_specs = (P("wide", "col"), P("wide", None, "col"), P("wide", None, "col"))
    return jax.shard_map(
        per_device, mesh=mesh, in_specs=in_specs, out_specs=out_specs, check_vma=False
    )
```

```python
import jax
import jax.numpy as jnp
from jax import lax
from jax.sharding import PartitionSpec as P

BLK = 128


PRECISE = lax.Precision.HIGH


def pick_blocks(source_rows, blocks):
    leading = source_rows.shape[0]
    tiled = source_rows.reshape(leading, source_rows.shape[1] // BLK, BLK)
    selected = jnp.take(tiled, blocks.reshape(-1), axis=1)
    return selected.reshape(leading, blocks.shape[0], blocks.shape[1] * BLK)


def exchange_sum(partial, axis):
    n = lax.axis_size(axis)
    chunk = partial.shape[0] // n
    parts = lax.all_to_all(partial.reshape((n, chunk) + partial.shape[1:]), axis, 0, 0, tiled=False)
    return parts.sum(0)


def exchange_gather(local, axis, dim):
    n = lax.axis_size(axis)
    stacked = jnp.broadcast_to(local[None], (n,) + local.shape)
    parts = lax.all_to_all(stacked, axis, 0, 0, tiled=False)
    parts = jnp.moveaxis(parts, 0, dim)
    return parts.reshape(local.shape[:dim] + (n * local.shape[dim],) + local.shape[dim + 1 :])


def chip_groups(n):
    return [[2 * x + core for x in range(n // 2)] for core in range(2)]


def pick_core(paired, index):
    taken = lax.dynamic_slice_in_dim(paired, index, 1, axis=1, allow_negative_indices=False)
    return taken.reshape(paired.shape[:1] + paired.shape[2:])


def col_sum(chunks, cores):
    n = lax.axis_size("col")
    paired = chunks.reshape((n // 2, 2) + chunks.shape[1:])
    mine = pick_core(paired, cores[0])
    other = pick_core(paired, cores[1])
    chip = mine + lax.ppermute(other, "col", [(d, d ^ 1) for d in range(n)])
    parts = lax.all_to_all(chip, "col", 0, 0, tiled=False, axis_index_groups=chip_groups(n))
    return parts.sum(0)


def col_halves(local):
    n = lax.axis_size("col")
    stacked = jnp.broadcast_to(local[None], (n // 2,) + local.shape)
    same = lax.all_to_all(stacked, "col", 0, 0, tiled=False, axis_index_groups=chip_groups(n))
    other = lax.ppermute(same, "col", [(d, d ^ 1) for d in range(n)])
    return same, other


def col_join(same, other, cores):
    both = jnp.where(cores[2], jnp.stack([same, other], 1), jnp.stack([other, same], 1))
    return both.reshape((-1,) + same.shape[1:])


def col_gather(local, cores):
    return col_join(*col_halves(local), cores)


def matmul(lhs, rhs, spec):
    return jnp.einsum(spec, lhs, rhs, precision=PRECISE, preferred_element_type=jnp.float32)


def level(z_local, update_partial, inverse, cores):
    n = lax.axis_size("col")
    update = col_sum(update_partial.reshape((n, -1) + update_partial.shape[1:]), cores)
    right_side = col_gather(z_local - update, cores)
    right_side = right_side.reshape((-1,) + right_side.shape[2:])
    return exchange_sum(matmul(right_side, inverse, "ski,kij->skj"), "wide")


def send_blocks(tiles, tables):
    other_mine, other_local, own_mine, own_local = tables
    n = 2 * other_mine.shape[0]
    other = jnp.where(other_mine[:, :, None, None], jnp.take(tiles, other_local, axis=0), 0.0)
    sent = lax.ppermute(other, "col", [(d, d ^ 1) for d in range(n)])
    own = jnp.where(own_mine[:, :, None, None], jnp.take(tiles, own_local, axis=0), 0.0)
    parts = lax.all_to_all(own + sent, "col", 0, 0, tiled=False, axis_index_groups=chip_groups(n))
    return parts.sum(0)


def by_core(table, cores):
    paired = table.reshape((table.shape[0] // 2, 2) + table.shape[1:])
    return (
        pick_core(paired, cores[1]),
        pick_core(paired, cores[0]),
    )


def slots_of(blocks, per_device):
    rows = blocks.shape[0]
    n_col = blocks.shape[1] // per_device
    return blocks.reshape(rows, n_col, per_device).transpose(1, 0, 2).reshape(n_col, rows * per_device)


def rows_of(received, rows, per_device):
    samples = received.shape[1]
    shaped = received.reshape(rows, per_device, samples, BLK).transpose(2, 0, 1, 3)
    return shaped.reshape(samples, rows, per_device * BLK)


def per_device(
    z_root,
    z_child,
    z_grand,
    inv_root,
    inv_child,
    inv_grand,
    panel_child,
    panel_grand,
    anc_child,
    anc_grand,
):
    n_col = lax.axis_size("col")
    child_list = anc_child.reshape(-1).astype(jnp.float32)
    grand_list = anc_grand.reshape(-1).astype(jnp.float32)
    width = z_root.shape[1]
    extra = jnp.stack(
        [jnp.pad(child_list, (0, width - child_list.shape[0])), jnp.pad(grand_list, (0, width - grand_list.shape[0]))]
        + [jnp.zeros((width,), jnp.float32)] * 6
    )
    here = lax.axis_index("col")
    cores = (here % 2, 1 - here % 2, here % 2 == 0)
    with_lists, here, cores = lax.optimization_barrier((jnp.concatenate([z_root, extra], axis=0)[None], here, cores))
    same, other = col_halves(with_lists[0])
    rows = z_root.shape[0]
    root_right = col_join(same[:, :rows], other[:, :rows], cores).reshape(-1, z_root.shape[1])
    got = col_join(same[:, rows : rows + 2], other[:, rows : rows + 2], cores).astype(jnp.int32)
    anc_child = got[:, 0, : anc_child.size].reshape((n_col,) + anc_child.shape).transpose(1, 0, 2).reshape(anc_child.shape[0], -1)
    anc_grand = got[:, 1, : anc_grand.size].reshape((n_col,) + anc_grand.shape).transpose(1, 0, 2).reshape(anc_grand.shape[0], -1)
    width = inv_root.shape[1]
    per_root = width // BLK
    kids, child_width = inv_child.shape[0], inv_child.shape[2]
    per_child = child_width // BLK

    child_slots = slots_of(anc_child, anc_child.shape[1] // n_col)
    child_owner, child_local = child_slots // per_root, child_slots % per_root
    grand_slots = slots_of(anc_grand, anc_grand.shape[1] // n_col)
    root_blocks = per_root * n_col
    is_root = grand_slots < root_blocks
    in_child = grand_slots - root_blocks
    child_block = in_child % (per_child * n_col)
    child_kid = in_child // (per_child * n_col)
    owner = jnp.where(is_root, grand_slots // per_root, child_block // per_child)
    local = jnp.where(is_root, grand_slots % per_root, per_root + child_kid * per_child + child_block % per_child)
    child_owner, owner = child_owner == here, owner == here
    child_tables = by_core(child_owner, cores) + by_core(child_local, cores)
    child_tables = (child_tables[0], child_tables[2], child_tables[1], child_tables[3])
    grand_tables = by_core(owner, cores) + by_core(local, cores)
    grand_tables = (grand_tables[0], grand_tables[2], grand_tables[1], grand_tables[3])
    root_right, child_tables, grand_tables, cores = lax.optimization_barrier(
        (root_right, child_tables, grand_tables, cores)
    )
    x_root = exchange_sum(matmul(root_right, inv_root, "si,ij->sj"), "wide")
    x_root, child_tables, grand_tables, cores = lax.optimization_barrier(
        (x_root, child_tables, grand_tables, cores)
    )
    root_tiles = x_root.reshape(x_root.shape[0], per_root, BLK).transpose(1, 0, 2)
    near_local = send_blocks(root_tiles, child_tables)
    near_local = rows_of(near_local, anc_child.shape[0], anc_child.shape[1] // n_col)
    near_rows = exchange_gather(near_local, "wide", 0)
    x_child = level(z_child, matmul(near_rows, panel_child, "ska,kaj->skj"), inv_child, cores)

    x_child, grand_tables, cores = lax.optimization_barrier((x_child, grand_tables, cores))
    child_tiles = x_child.reshape(x_child.shape[0], kids * per_child, BLK).transpose(1, 0, 2)
    all_tiles = jnp.concatenate([root_tiles, child_tiles], axis=0)
    far_local = send_blocks(all_tiles, grand_tables)
    far_local = rows_of(far_local, anc_grand.shape[0], anc_grand.shape[1] // n_col)
    far_rows = exchange_gather(far_local, "wide", 0)
    x_grand = level(z_grand, matmul(far_rows, panel_grand, "sga,gaj->sgj"), inv_grand, cores)
    return (x_root, x_child, x_grand)


def solution(mesh):
    in_specs = (
        P("col", "wide"),
        P("col", None, "wide"),
        P("col", None, "wide"),
        P("wide", "col"),
        P(None, "wide", "col"),
        P(None, "wide", "col"),
        P(None, "col", "wide"),
        P(None, "col", "wide"),
        P(None, "col"),
        P(None, "col"),
    )
    out_specs = (P("wide", "col"), P("wide", None, "col"), P("wide", None, "col"))
    return jax.shard_map(
        per_device, mesh=mesh, in_specs=in_specs, out_specs=out_specs, check_vma=False
    )
```

```python
import jax
import jax.numpy as jnp
from jax import lax
from jax.sharding import PartitionSpec as P

BLK = 128


PRECISE = lax.Precision.HIGH


def pick_blocks(source_rows, blocks):
    leading = source_rows.shape[0]
    tiled = source_rows.reshape(leading, source_rows.shape[1] // BLK, BLK)
    selected = jnp.take(tiled, blocks.reshape(-1), axis=1)
    return selected.reshape(leading, blocks.shape[0], blocks.shape[1] * BLK)


def add_up(parts):
    n = parts.shape[0]
    grouped = parts.reshape((n // 4, 4) + parts.shape[1:]).sum(1)
    return lax.optimization_barrier(grouped).sum(0)


def exchange_sum(partial, axis):
    n = lax.axis_size(axis)
    chunk = partial.shape[0] // n
    parts = lax.all_to_all(partial.reshape((n, chunk) + partial.shape[1:]), axis, 0, 0, tiled=False)
    return add_up(parts)


def exchange_gather(local, axis, dim):
    n = lax.axis_size(axis)
    stacked = jnp.broadcast_to(local[None], (n,) + local.shape)
    parts = lax.all_to_all(stacked, axis, 0, 0, tiled=False)
    parts = jnp.moveaxis(parts, 0, dim)
    return parts.reshape(local.shape[:dim] + (n * local.shape[dim],) + local.shape[dim + 1 :])


def chip_groups(n):
    return [[2 * x + core for x in range(n // 2)] for core in range(2)]


def pick_core(paired, index):
    taken = lax.dynamic_slice_in_dim(paired, index, 1, axis=1, allow_negative_indices=False)
    return taken.reshape(paired.shape[:1] + paired.shape[2:])


def col_sum(chunks, cores):
    n = lax.axis_size("col")
    paired = chunks.reshape((n // 2, 2) + chunks.shape[1:])
    mine = pick_core(paired, cores[0])
    other = pick_core(paired, cores[1])
    chip = mine + lax.ppermute(other, "col", [(d, d ^ 1) for d in range(n)])
    parts = lax.all_to_all(chip, "col", 0, 0, tiled=False, axis_index_groups=chip_groups(n))
    return parts.sum(0)


def col_halves(local):
    n = lax.axis_size("col")
    stacked = jnp.broadcast_to(local[None], (n // 2,) + local.shape)
    same = lax.all_to_all(stacked, "col", 0, 0, tiled=False, axis_index_groups=chip_groups(n))
    other = lax.ppermute(same, "col", [(d, d ^ 1) for d in range(n)])
    return same, other


def col_join(same, other, cores):
    both = jnp.where(cores[2], jnp.stack([same, other], 1), jnp.stack([other, same], 1))
    return both.reshape((-1,) + same.shape[1:])


def col_gather(local, cores):
    return col_join(*col_halves(local), cores)


def matmul(lhs, rhs, spec):
    return jnp.einsum(spec, lhs, rhs, precision=PRECISE, preferred_element_type=jnp.float32)


def level(z_local, update_partial, inverse, cores):
    n = lax.axis_size("col")
    update = col_sum(update_partial.reshape((n, -1) + update_partial.shape[1:]), cores)
    right_side = col_gather(z_local - update, cores)
    right_side = right_side.reshape((-1,) + right_side.shape[2:])
    return exchange_sum(matmul(right_side, inverse, "ski,kij->skj"), "wide")


def send_blocks(tiles, tables):
    other_mine, other_local, own_mine, own_local = tables
    n = 2 * other_mine.shape[0]
    other = jnp.where(other_mine[:, :, None, None], jnp.take(tiles, other_local, axis=0), 0.0)
    sent = lax.ppermute(other, "col", [(d, d ^ 1) for d in range(n)])
    own = jnp.where(own_mine[:, :, None, None], jnp.take(tiles, own_local, axis=0), 0.0)
    parts = lax.all_to_all(own + sent, "col", 0, 0, tiled=False, axis_index_groups=chip_groups(n))
    return parts.sum(0)


def by_core(table, cores):
    paired = table.reshape((table.shape[0] // 2, 2) + table.shape[1:])
    return (
        pick_core(paired, cores[1]),
        pick_core(paired, cores[0]),
    )


def slots_of(blocks, per_device):
    rows = blocks.shape[0]
    n_col = blocks.shape[1] // per_device
    return blocks.reshape(rows, n_col, per_device).transpose(1, 0, 2).reshape(n_col, rows * per_device)


def rows_of(received, rows, per_device):
    samples = received.shape[1]
    shaped = received.reshape(rows, per_device, samples, BLK).transpose(2, 0, 1, 3)
    return shaped.reshape(samples, rows, per_device * BLK)


def per_device(
    z_root,
    z_child,
    z_grand,
    inv_root,
    inv_child,
    inv_grand,
    panel_child,
    panel_grand,
    anc_child,
    anc_grand,
):
    n_col = lax.axis_size("col")
    child_list = anc_child.reshape(-1).astype(jnp.float32)
    grand_list = anc_grand.reshape(-1).astype(jnp.float32)
    width = z_root.shape[1]
    extra = jnp.stack(
        [jnp.pad(child_list, (0, width - child_list.shape[0])), jnp.pad(grand_list, (0, width - grand_list.shape[0]))]
        + [jnp.zeros((width,), jnp.float32)] * 6
    )
    here = lax.axis_index("col")
    cores = (here % 2, 1 - here % 2, here % 2 == 0)
    with_lists, here, cores = lax.optimization_barrier((jnp.concatenate([z_root, extra], axis=0)[None], here, cores))
    same, other = col_halves(with_lists[0])
    rows = z_root.shape[0]
    root_right = col_join(same[:, :rows], other[:, :rows], cores).reshape(-1, z_root.shape[1])
    got = col_join(same[:, rows : rows + 2], other[:, rows : rows + 2], cores).astype(jnp.int32)
    anc_child = got[:, 0, : anc_child.size].reshape((n_col,) + anc_child.shape).transpose(1, 0, 2).reshape(anc_child.shape[0], -1)
    anc_grand = got[:, 1, : anc_grand.size].reshape((n_col,) + anc_grand.shape).transpose(1, 0, 2).reshape(anc_grand.shape[0], -1)
    width = inv_root.shape[1]
    per_root = width // BLK
    kids, child_width = inv_child.shape[0], inv_child.shape[2]
    per_child = child_width // BLK

    child_slots = slots_of(anc_child, anc_child.shape[1] // n_col)
    child_owner, child_local = child_slots // per_root, child_slots % per_root
    grand_slots = slots_of(anc_grand, anc_grand.shape[1] // n_col)
    root_blocks = per_root * n_col
    is_root = grand_slots < root_blocks
    in_child = grand_slots - root_blocks
    child_block = in_child % (per_child * n_col)
    child_kid = in_child // (per_child * n_col)
    owner = jnp.where(is_root, grand_slots // per_root, child_block // per_child)
    local = jnp.where(is_root, grand_slots % per_root, per_root + child_kid * per_child + child_block % per_child)
    child_owner, owner = child_owner == here, owner == here
    child_tables = by_core(child_owner, cores) + by_core(child_local, cores)
    child_tables = (child_tables[0], child_tables[2], child_tables[1], child_tables[3])
    grand_tables = by_core(owner, cores) + by_core(local, cores)
    grand_tables = (grand_tables[0], grand_tables[2], grand_tables[1], grand_tables[3])
    root_right, child_tables, grand_tables, cores = lax.optimization_barrier(
        (root_right, child_tables, grand_tables, cores)
    )
    x_root = exchange_sum(matmul(root_right, inv_root, "si,ij->sj"), "wide")
    x_root, child_tables, grand_tables, cores = lax.optimization_barrier(
        (x_root, child_tables, grand_tables, cores)
    )
    root_tiles = x_root.reshape(x_root.shape[0], per_root, BLK).transpose(1, 0, 2)
    near_local = send_blocks(root_tiles, child_tables)
    near_local = rows_of(near_local, anc_child.shape[0], anc_child.shape[1] // n_col)
    near_rows = exchange_gather(near_local, "wide", 0)
    x_child = level(z_child, matmul(near_rows, panel_child, "ska,kaj->skj"), inv_child, cores)

    x_child, grand_tables, cores = lax.optimization_barrier((x_child, grand_tables, cores))
    child_tiles = x_child.reshape(x_child.shape[0], kids * per_child, BLK).transpose(1, 0, 2)
    all_tiles = jnp.concatenate([root_tiles, child_tiles], axis=0)
    far_local = send_blocks(all_tiles, grand_tables)
    far_local = rows_of(far_local, anc_grand.shape[0], anc_grand.shape[1] // n_col)
    far_rows = exchange_gather(far_local, "wide", 0)
    x_grand = level(z_grand, matmul(far_rows, panel_grand, "sga,gaj->sgj"), inv_grand, cores)
    return (x_root, x_child, x_grand)


def solution(mesh):
    in_specs = (
        P("col", "wide"),
        P("col", None, "wide"),
        P("col", None, "wide"),
        P("wide", "col"),
        P(None, "wide", "col"),
        P(None, "wide", "col"),
        P(None, "col", "wide"),
        P(None, "col", "wide"),
        P(None, "col"),
        P(None, "col"),
    )
    out_specs = (P("wide", "col"), P("wide", None, "col"), P("wide", None, "col"))
    return jax.shard_map(
        per_device, mesh=mesh, in_specs=in_specs, out_specs=out_specs, check_vma=False
    )
```

```python
import jax
import jax.numpy as jnp
from jax import lax
from jax.sharding import PartitionSpec as P

BLK = 128


PRECISE = lax.Precision.HIGH


def pick_blocks(source_rows, blocks):
    leading = source_rows.shape[0]
    tiled = source_rows.reshape(leading, source_rows.shape[1] // BLK, BLK)
    selected = jnp.take(tiled, blocks.reshape(-1), axis=1)
    return selected.reshape(leading, blocks.shape[0], blocks.shape[1] * BLK)


def add_up(parts):
    n = parts.shape[0]
    grouped = parts.reshape((n // 4, 4) + parts.shape[1:]).sum(1)
    return lax.optimization_barrier(grouped).sum(0)


def exchange_sum(partial, axis):
    n = lax.axis_size(axis)
    chunk = partial.shape[0] // n
    parts = lax.all_to_all(partial.reshape((n, chunk) + partial.shape[1:]), axis, 0, 0, tiled=False)
    return add_up(parts)


def exchange_gather(local, axis, dim):
    n = lax.axis_size(axis)
    stacked = jnp.broadcast_to(local[None], (n,) + local.shape)
    parts = lax.all_to_all(stacked, axis, 0, 0, tiled=False)
    parts = jnp.moveaxis(parts, 0, dim)
    return parts.reshape(local.shape[:dim] + (n * local.shape[dim],) + local.shape[dim + 1 :])


def chip_groups(n):
    return [[2 * x + core for x in range(n // 2)] for core in range(2)]


def pick_core(paired, index):
    taken = lax.dynamic_slice_in_dim(paired, index, 1, axis=1, allow_negative_indices=False)
    return taken.reshape(paired.shape[:1] + paired.shape[2:])


def col_sum(chunks, cores):
    n = lax.axis_size("col")
    paired = chunks.reshape((n // 2, 2) + chunks.shape[1:])
    mine = pick_core(paired, cores[0])
    other = pick_core(paired, cores[1])
    chip = mine + lax.ppermute(other, "col", [(d, d ^ 1) for d in range(n)])
    parts = lax.all_to_all(chip, "col", 0, 0, tiled=False, axis_index_groups=chip_groups(n))
    return parts.sum(0)


def col_halves(local):
    n = lax.axis_size("col")
    stacked = jnp.broadcast_to(local[None], (n // 2,) + local.shape)
    same = lax.all_to_all(stacked, "col", 0, 0, tiled=False, axis_index_groups=chip_groups(n))
    other = lax.ppermute(same, "col", [(d, d ^ 1) for d in range(n)])
    return same, other


def col_join(same, other, cores):
    both = jnp.where(cores[2], jnp.stack([same, other], 1), jnp.stack([other, same], 1))
    return both.reshape((-1,) + same.shape[1:])


def col_gather(local, cores):
    return col_join(*col_halves(local), cores)


def matmul(lhs, rhs, spec):
    return jnp.einsum(spec, lhs, rhs, precision=PRECISE, preferred_element_type=jnp.float32)


def level(z_local, near_rows, panel, spec, inverse, cores):
    n = lax.axis_size("col")
    paired = near_rows.reshape((n // 2, 2, -1) + near_rows.shape[1:])
    other = pick_core(paired, cores[1])
    other = matmul(other.reshape((-1,) + other.shape[2:]), panel, spec)
    sent = lax.ppermute(other.reshape((n // 2, -1) + other.shape[1:]), "col", [(d, d ^ 1) for d in range(n)])
    mine = pick_core(paired, cores[0])
    mine = matmul(mine.reshape((-1,) + mine.shape[2:]), panel, spec)
    chip = mine.reshape(sent.shape) + sent
    update = lax.all_to_all(chip, "col", 0, 0, tiled=False, axis_index_groups=chip_groups(n)).sum(0)
    right_side = col_gather(z_local - update, cores)
    right_side = right_side.reshape((-1,) + right_side.shape[2:])
    return exchange_sum(matmul(right_side, inverse, "ski,kij->skj"), "wide")


def send_blocks(tiles, tables):
    other_mine, other_local, own_mine, own_local = tables
    n = 2 * other_mine.shape[0]
    other = jnp.where(other_mine[:, :, None, None], jnp.take(tiles, other_local, axis=0), 0.0)
    sent = lax.ppermute(other, "col", [(d, d ^ 1) for d in range(n)])
    own = jnp.where(own_mine[:, :, None, None], jnp.take(tiles, own_local, axis=0), 0.0)
    parts = lax.all_to_all(own + sent, "col", 0, 0, tiled=False, axis_index_groups=chip_groups(n))
    return parts.sum(0)


def by_core(table, cores):
    paired = table.reshape((table.shape[0] // 2, 2) + table.shape[1:])
    return (
        pick_core(paired, cores[1]),
        pick_core(paired, cores[0]),
    )


def slots_of(blocks, per_device):
    rows = blocks.shape[0]
    n_col = blocks.shape[1] // per_device
    return blocks.reshape(rows, n_col, per_device).transpose(1, 0, 2).reshape(n_col, rows * per_device)


def rows_of(received, rows, per_device):
    samples = received.shape[1]
    shaped = received.reshape(rows, per_device, samples, BLK).transpose(2, 0, 1, 3)
    return shaped.reshape(samples, rows, per_device * BLK)


def per_device(
    z_root,
    z_child,
    z_grand,
    inv_root,
    inv_child,
    inv_grand,
    panel_child,
    panel_grand,
    anc_child,
    anc_grand,
):
    n_col = lax.axis_size("col")
    child_list = anc_child.reshape(-1).astype(jnp.float32)
    grand_list = anc_grand.reshape(-1).astype(jnp.float32)
    width = z_root.shape[1]
    extra = jnp.stack(
        [jnp.pad(child_list, (0, width - child_list.shape[0])), jnp.pad(grand_list, (0, width - grand_list.shape[0]))]
        + [jnp.zeros((width,), jnp.float32)] * 6
    )
    here = lax.axis_index("col")
    cores = (here % 2, 1 - here % 2, here % 2 == 0)
    with_lists, here, cores = lax.optimization_barrier((jnp.concatenate([z_root, extra], axis=0)[None], here, cores))
    same, other = col_halves(with_lists[0])
    rows = z_root.shape[0]
    root_right = col_join(same[:, :rows], other[:, :rows], cores).reshape(-1, z_root.shape[1])
    got = col_join(same[:, rows : rows + 2], other[:, rows : rows + 2], cores).astype(jnp.int32)
    anc_child = got[:, 0, : anc_child.size].reshape((n_col,) + anc_child.shape).transpose(1, 0, 2).reshape(anc_child.shape[0], -1)
    anc_grand = got[:, 1, : anc_grand.size].reshape((n_col,) + anc_grand.shape).transpose(1, 0, 2).reshape(anc_grand.shape[0], -1)
    width = inv_root.shape[1]
    per_root = width // BLK
    kids, child_width = inv_child.shape[0], inv_child.shape[2]
    per_child = child_width // BLK

    child_slots = slots_of(anc_child, anc_child.shape[1] // n_col)
    child_owner, child_local = child_slots // per_root, child_slots % per_root
    grand_slots = slots_of(anc_grand, anc_grand.shape[1] // n_col)
    root_blocks = per_root * n_col
    is_root = grand_slots < root_blocks
    in_child = grand_slots - root_blocks
    child_block = in_child % (per_child * n_col)
    child_kid = in_child // (per_child * n_col)
    owner = jnp.where(is_root, grand_slots // per_root, child_block // per_child)
    local = jnp.where(is_root, grand_slots % per_root, per_root + child_kid * per_child + child_block % per_child)
    child_owner, owner = child_owner == here, owner == here
    child_tables = by_core(child_owner, cores) + by_core(child_local, cores)
    child_tables = (child_tables[0], child_tables[2], child_tables[1], child_tables[3])
    grand_tables = by_core(owner, cores) + by_core(local, cores)
    grand_tables = (grand_tables[0], grand_tables[2], grand_tables[1], grand_tables[3])
    root_right, child_tables, grand_tables, cores = lax.optimization_barrier(
        (root_right, child_tables, grand_tables, cores)
    )
    x_root = exchange_sum(matmul(root_right, inv_root, "si,ij->sj"), "wide")
    x_root, child_tables, grand_tables, cores = lax.optimization_barrier(
        (x_root, child_tables, grand_tables, cores)
    )
    root_tiles = x_root.reshape(x_root.shape[0], per_root, BLK).transpose(1, 0, 2)
    near_local = send_blocks(root_tiles, child_tables)
    near_local = rows_of(near_local, anc_child.shape[0], anc_child.shape[1] // n_col)
    near_rows = exchange_gather(near_local, "wide", 0)
    x_child = level(z_child, near_rows, panel_child, "ska,kaj->skj", inv_child, cores)

    x_child, grand_tables, cores = lax.optimization_barrier((x_child, grand_tables, cores))
    child_tiles = x_child.reshape(x_child.shape[0], kids * per_child, BLK).transpose(1, 0, 2)
    all_tiles = jnp.concatenate([root_tiles, child_tiles], axis=0)
    far_local = send_blocks(all_tiles, grand_tables)
    far_local = rows_of(far_local, anc_grand.shape[0], anc_grand.shape[1] // n_col)
    far_rows = exchange_gather(far_local, "wide", 0)
    x_grand = level(z_grand, far_rows, panel_grand, "sga,gaj->sgj", inv_grand, cores)
    return (x_root, x_child, x_grand)


def solution(mesh):
    in_specs = (
        P("col", "wide"),
        P("col", None, "wide"),
        P("col", None, "wide"),
        P("wide", "col"),
        P(None, "wide", "col"),
        P(None, "wide", "col"),
        P(None, "col", "wide"),
        P(None, "col", "wide"),
        P(None, "col"),
        P(None, "col"),
    )
    out_specs = (P("wide", "col"), P("wide", None, "col"), P("wide", None, "col"))
    return jax.shard_map(
        per_device, mesh=mesh, in_specs=in_specs, out_specs=out_specs, check_vma=False
    )
```

```python
import jax
import jax.numpy as jnp
from jax import lax
from jax.sharding import PartitionSpec as P

BLK = 128


PRECISE = lax.Precision.HIGH


def pick_blocks(source_rows, blocks):
    leading = source_rows.shape[0]
    tiled = source_rows.reshape(leading, source_rows.shape[1] // BLK, BLK)
    selected = jnp.take(tiled, blocks.reshape(-1), axis=1)
    return selected.reshape(leading, blocks.shape[0], blocks.shape[1] * BLK)


def add_up(parts):
    n = parts.shape[0]
    grouped = parts.reshape((n // 4, 4) + parts.shape[1:]).sum(1)
    return lax.optimization_barrier(grouped).sum(0)


def exchange_sum(partial, axis):
    n = lax.axis_size(axis)
    chunk = partial.shape[0] // n
    parts = lax.all_to_all(partial.reshape((n, chunk) + partial.shape[1:]), axis, 0, 0, tiled=False)
    return add_up(parts)


def exchange_gather(local, axis, dim):
    n = lax.axis_size(axis)
    stacked = jnp.broadcast_to(local[None], (n,) + local.shape)
    parts = lax.all_to_all(stacked, axis, 0, 0, tiled=False)
    parts = jnp.moveaxis(parts, 0, dim)
    return parts.reshape(local.shape[:dim] + (n * local.shape[dim],) + local.shape[dim + 1 :])


def chip_groups(n):
    return [[2 * x + core for x in range(n // 2)] for core in range(2)]


def pick_core(paired, index):
    taken = lax.dynamic_slice_in_dim(paired, index, 1, axis=1, allow_negative_indices=False)
    return taken.reshape(paired.shape[:1] + paired.shape[2:])


def col_sum(chunks, cores):
    n = lax.axis_size("col")
    paired = chunks.reshape((n // 2, 2) + chunks.shape[1:])
    mine = pick_core(paired, cores[0])
    other = pick_core(paired, cores[1])
    chip = mine + lax.ppermute(other, "col", [(d, d ^ 1) for d in range(n)])
    parts = lax.all_to_all(chip, "col", 0, 0, tiled=False, axis_index_groups=chip_groups(n))
    return parts.sum(0)


def col_halves(local):
    n = lax.axis_size("col")
    stacked = jnp.broadcast_to(local[None], (n // 2,) + local.shape)
    same = lax.all_to_all(stacked, "col", 0, 0, tiled=False, axis_index_groups=chip_groups(n))
    other = lax.ppermute(same, "col", [(d, d ^ 1) for d in range(n)])
    return same, other


def col_join(same, other, cores):
    both = jnp.where(cores[2], jnp.stack([same, other], 1), jnp.stack([other, same], 1))
    return both.reshape((-1,) + same.shape[1:])


def col_gather(local, cores):
    return col_join(*col_halves(local), cores)


def matmul(lhs, rhs, spec):
    return jnp.einsum(spec, lhs, rhs, precision=PRECISE, preferred_element_type=jnp.float32)


def level(z_local, near_rows, panel, spec, inverse, cores):
    n = lax.axis_size("col")
    paired = near_rows.reshape((n // 2, 2, -1) + near_rows.shape[1:])
    other = pick_core(paired, cores[1])
    other = matmul(other.reshape((-1,) + other.shape[2:]), panel, spec)
    sent = lax.ppermute(other.reshape((n // 2, -1) + other.shape[1:]), "col", [(d, d ^ 1) for d in range(n)])
    mine = pick_core(paired, cores[0])
    mine = matmul(mine.reshape((-1,) + mine.shape[2:]), panel, spec)
    chip = mine.reshape(sent.shape) + sent
    update = lax.all_to_all(chip, "col", 0, 0, tiled=False, axis_index_groups=chip_groups(n)).sum(0)
    same, other = col_halves(z_local - update)
    own = matmul(same.reshape((-1,) + same.shape[2:]), inverse, "ski,kij->skj")
    far = matmul(other.reshape((-1,) + other.shape[2:]), inverse, "ski,kij->skj")
    partial = col_join(own.reshape(same.shape[:2] + own.shape[1:]), far.reshape(other.shape[:2] + far.shape[1:]), cores)
    return exchange_sum(partial.reshape((-1,) + partial.shape[2:]), "wide")


def send_blocks(tiles, tables):
    other_mine, other_local, own_mine, own_local = tables
    n = 2 * other_mine.shape[0]
    other = jnp.where(other_mine[:, :, None, None], jnp.take(tiles, other_local, axis=0), 0.0)
    sent = lax.ppermute(other, "col", [(d, d ^ 1) for d in range(n)])
    own = jnp.where(own_mine[:, :, None, None], jnp.take(tiles, own_local, axis=0), 0.0)
    parts = lax.all_to_all(own + sent, "col", 0, 0, tiled=False, axis_index_groups=chip_groups(n))
    return parts.sum(0)


def by_core(table, cores):
    paired = table.reshape((table.shape[0] // 2, 2) + table.shape[1:])
    return (
        pick_core(paired, cores[1]),
        pick_core(paired, cores[0]),
    )


def slots_of(blocks, per_device):
    rows = blocks.shape[0]
    n_col = blocks.shape[1] // per_device
    return blocks.reshape(rows, n_col, per_device).transpose(1, 0, 2).reshape(n_col, rows * per_device)


def rows_of(received, rows, per_device):
    samples = received.shape[1]
    shaped = received.reshape(rows, per_device, samples, BLK).transpose(2, 0, 1, 3)
    return shaped.reshape(samples, rows, per_device * BLK)


def per_device(
    z_root,
    z_child,
    z_grand,
    inv_root,
    inv_child,
    inv_grand,
    panel_child,
    panel_grand,
    anc_child,
    anc_grand,
):
    n_col = lax.axis_size("col")
    child_list = anc_child.reshape(-1).astype(jnp.float32)
    grand_list = anc_grand.reshape(-1).astype(jnp.float32)
    width = z_root.shape[1]
    extra = jnp.stack(
        [jnp.pad(child_list, (0, width - child_list.shape[0])), jnp.pad(grand_list, (0, width - grand_list.shape[0]))]
        + [jnp.zeros((width,), jnp.float32)] * 6
    )
    here = lax.axis_index("col")
    cores = (here % 2, 1 - here % 2, here % 2 == 0)
    with_lists, here, cores = lax.optimization_barrier((jnp.concatenate([z_root, extra], axis=0)[None], here, cores))
    same, other = col_halves(with_lists[0])
    rows = z_root.shape[0]
    root_right = col_join(same[:, :rows], other[:, :rows], cores).reshape(-1, z_root.shape[1])
    got = col_join(same[:, rows : rows + 2], other[:, rows : rows + 2], cores).astype(jnp.int32)
    anc_child = got[:, 0, : anc_child.size].reshape((n_col,) + anc_child.shape).transpose(1, 0, 2).reshape(anc_child.shape[0], -1)
    anc_grand = got[:, 1, : anc_grand.size].reshape((n_col,) + anc_grand.shape).transpose(1, 0, 2).reshape(anc_grand.shape[0], -1)
    width = inv_root.shape[1]
    per_root = width // BLK
    kids, child_width = inv_child.shape[0], inv_child.shape[2]
    per_child = child_width // BLK

    child_slots = slots_of(anc_child, anc_child.shape[1] // n_col)
    child_owner, child_local = child_slots // per_root, child_slots % per_root
    grand_slots = slots_of(anc_grand, anc_grand.shape[1] // n_col)
    root_blocks = per_root * n_col
    is_root = grand_slots < root_blocks
    in_child = grand_slots - root_blocks
    child_block = in_child % (per_child * n_col)
    child_kid = in_child // (per_child * n_col)
    owner = jnp.where(is_root, grand_slots // per_root, child_block // per_child)
    local = jnp.where(is_root, grand_slots % per_root, per_root + child_kid * per_child + child_block % per_child)
    child_owner, owner = child_owner == here, owner == here
    child_tables = by_core(child_owner, cores) + by_core(child_local, cores)
    child_tables = (child_tables[0], child_tables[2], child_tables[1], child_tables[3])
    grand_tables = by_core(owner, cores) + by_core(local, cores)
    grand_tables = (grand_tables[0], grand_tables[2], grand_tables[1], grand_tables[3])
    root_right, child_tables, grand_tables, cores = lax.optimization_barrier(
        (root_right, child_tables, grand_tables, cores)
    )
    x_root = exchange_sum(matmul(root_right, inv_root, "si,ij->sj"), "wide")
    x_root, child_tables, grand_tables, cores = lax.optimization_barrier(
        (x_root, child_tables, grand_tables, cores)
    )
    root_tiles = x_root.reshape(x_root.shape[0], per_root, BLK).transpose(1, 0, 2)
    near_local = send_blocks(root_tiles, child_tables)
    near_local = rows_of(near_local, anc_child.shape[0], anc_child.shape[1] // n_col)
    near_rows = exchange_gather(near_local, "wide", 0)
    x_child = level(z_child, near_rows, panel_child, "ska,kaj->skj", inv_child, cores)

    x_child, grand_tables, cores = lax.optimization_barrier((x_child, grand_tables, cores))
    child_tiles = x_child.reshape(x_child.shape[0], kids * per_child, BLK).transpose(1, 0, 2)
    all_tiles = jnp.concatenate([root_tiles, child_tiles], axis=0)
    far_local = send_blocks(all_tiles, grand_tables)
    far_local = rows_of(far_local, anc_grand.shape[0], anc_grand.shape[1] // n_col)
    far_rows = exchange_gather(far_local, "wide", 0)
    x_grand = level(z_grand, far_rows, panel_grand, "sga,gaj->sgj", inv_grand, cores)
    return (x_root, x_child, x_grand)


def solution(mesh):
    in_specs = (
        P("col", "wide"),
        P("col", None, "wide"),
        P("col", None, "wide"),
        P("wide", "col"),
        P(None, "wide", "col"),
        P(None, "wide", "col"),
        P(None, "col", "wide"),
        P(None, "col", "wide"),
        P(None, "col"),
        P(None, "col"),
    )
    out_specs = (P("wide", "col"), P("wide", None, "col"), P("wide", None, "col"))
    return jax.shard_map(
        per_device, mesh=mesh, in_specs=in_specs, out_specs=out_specs, check_vma=False
    )
```

```python
import jax
import jax.numpy as jnp
from jax import lax
from jax.sharding import PartitionSpec as P

BLK = 128


PRECISE = lax.Precision.HIGH


def pick_blocks(source_rows, blocks):
    leading = source_rows.shape[0]
    tiled = source_rows.reshape(leading, source_rows.shape[1] // BLK, BLK)
    selected = jnp.take(tiled, blocks.reshape(-1), axis=1)
    return selected.reshape(leading, blocks.shape[0], blocks.shape[1] * BLK)


def add_up(parts):
    n = parts.shape[0]
    grouped = parts.reshape((n // 4, 4) + parts.shape[1:]).sum(1)
    return lax.optimization_barrier(grouped).sum(0)


def exchange_sum(partial, axis):
    n = lax.axis_size(axis)
    chunk = partial.shape[0] // n
    parts = lax.all_to_all(partial.reshape((n, chunk) + partial.shape[1:]), axis, 0, 0, tiled=False)
    return add_up(parts)


def exchange_gather(local, axis, dim):
    n = lax.axis_size(axis)
    stacked = jnp.broadcast_to(local[None], (n,) + local.shape)
    parts = lax.all_to_all(stacked, axis, 0, 0, tiled=False)
    parts = jnp.moveaxis(parts, 0, dim)
    return parts.reshape(local.shape[:dim] + (n * local.shape[dim],) + local.shape[dim + 1 :])


def chip_groups(n):
    return [[2 * x + core for x in range(n // 2)] for core in range(2)]


def pick_core(paired, index):
    taken = lax.dynamic_slice_in_dim(paired, index, 1, axis=1, allow_negative_indices=False)
    return taken.reshape(paired.shape[:1] + paired.shape[2:])


def col_sum(chunks, cores):
    n = lax.axis_size("col")
    paired = chunks.reshape((n // 2, 2) + chunks.shape[1:])
    mine = pick_core(paired, cores[0])
    other = pick_core(paired, cores[1])
    chip = mine + lax.ppermute(other, "col", [(d, d ^ 1) for d in range(n)])
    parts = lax.all_to_all(chip, "col", 0, 0, tiled=False, axis_index_groups=chip_groups(n))
    return parts.sum(0)


def col_halves(local):
    n = lax.axis_size("col")
    stacked = jnp.broadcast_to(local[None], (n // 2,) + local.shape)
    same = lax.all_to_all(stacked, "col", 0, 0, tiled=False, axis_index_groups=chip_groups(n))
    other = lax.ppermute(same, "col", [(d, d ^ 1) for d in range(n)])
    return same, other


def col_join(same, other, cores):
    both = jnp.where(cores[2], jnp.stack([same, other], 1), jnp.stack([other, same], 1))
    return both.reshape((-1,) + same.shape[1:])


def col_gather(local, cores):
    return col_join(*col_halves(local), cores)


def matmul(lhs, rhs, spec):
    return jnp.einsum(spec, lhs, rhs, precision=PRECISE, preferred_element_type=jnp.float32)


def level(z_local, near_rows, panel, spec, inverse, cores):
    n = lax.axis_size("col")
    paired = near_rows.reshape((n // 2, 2, -1) + near_rows.shape[1:])
    other = pick_core(paired, cores[1])
    other = matmul(other.reshape((-1,) + other.shape[2:]), panel, spec)
    sent = lax.ppermute(other.reshape((n // 2, -1) + other.shape[1:]), "col", [(d, d ^ 1) for d in range(n)])
    mine = pick_core(paired, cores[0])
    mine = matmul(mine.reshape((-1,) + mine.shape[2:]), panel, spec)
    chip = mine.reshape(sent.shape) + sent
    update = lax.all_to_all(chip, "col", 0, 0, tiled=False, axis_index_groups=chip_groups(n)).sum(0)
    same, other = col_halves(z_local - update)
    own = matmul(same.reshape((-1,) + same.shape[2:]), inverse, "ski,kij->skj")
    far = matmul(other.reshape((-1,) + other.shape[2:]), inverse, "ski,kij->skj")
    partial = col_join(own.reshape(same.shape[:2] + own.shape[1:]), far.reshape(other.shape[:2] + far.shape[1:]), cores)
    return exchange_sum(partial.reshape((-1,) + partial.shape[2:]), "wide")


def send_blocks(tiles, tables):
    other_mine, other_local, own_mine, own_local = tables
    n = 2 * other_mine.shape[0]
    other = jnp.where(other_mine[:, :, None, None], jnp.take(tiles, other_local, axis=0), 0.0)
    sent = lax.ppermute(other, "col", [(d, d ^ 1) for d in range(n)])
    own = jnp.where(own_mine[:, :, None, None], jnp.take(tiles, own_local, axis=0), 0.0)
    parts = lax.all_to_all(own + sent, "col", 0, 0, tiled=False, axis_index_groups=chip_groups(n))
    return parts.sum(0)


def by_core(table, cores):
    paired = table.reshape((table.shape[0] // 2, 2) + table.shape[1:])
    return (
        pick_core(paired, cores[1]),
        pick_core(paired, cores[0]),
    )


def slots_of(blocks, per_device):
    rows = blocks.shape[0]
    n_col = blocks.shape[1] // per_device
    return blocks.reshape(rows, n_col, per_device).transpose(1, 0, 2).reshape(n_col, rows * per_device)


def rows_of(received, rows, per_device):
    samples = received.shape[1]
    shaped = received.reshape(rows, per_device, samples, BLK).transpose(2, 0, 1, 3)
    return shaped.reshape(samples, rows, per_device * BLK)


def per_device(
    z_root,
    z_child,
    z_grand,
    inv_root,
    inv_child,
    inv_grand,
    panel_child,
    panel_grand,
    anc_child,
    anc_grand,
):
    n_col = lax.axis_size("col")
    child_list = anc_child.reshape(-1).astype(jnp.float32)
    grand_list = anc_grand.reshape(-1).astype(jnp.float32)
    width = z_root.shape[1]
    extra = jnp.stack(
        [jnp.pad(child_list, (0, width - child_list.shape[0])), jnp.pad(grand_list, (0, width - grand_list.shape[0]))]
        + [jnp.zeros((width,), jnp.float32)] * 6
    )
    here = lax.axis_index("col")
    cores = (here % 2, 1 - here % 2, here % 2 == 0)
    with_lists, here, cores = lax.optimization_barrier((jnp.concatenate([z_root, extra], axis=0)[None], here, cores))
    same, other = col_halves(with_lists[0])
    rows = z_root.shape[0]
    root_same, root_other = same[:, :rows], other[:, :rows]
    got = col_join(same[:, rows : rows + 2], other[:, rows : rows + 2], cores).astype(jnp.int32)
    anc_child = got[:, 0, : anc_child.size].reshape((n_col,) + anc_child.shape).transpose(1, 0, 2).reshape(anc_child.shape[0], -1)
    anc_grand = got[:, 1, : anc_grand.size].reshape((n_col,) + anc_grand.shape).transpose(1, 0, 2).reshape(anc_grand.shape[0], -1)
    width = inv_root.shape[1]
    per_root = width // BLK
    kids, child_width = inv_child.shape[0], inv_child.shape[2]
    per_child = child_width // BLK

    child_slots = slots_of(anc_child, anc_child.shape[1] // n_col)
    child_owner, child_local = child_slots // per_root, child_slots % per_root
    grand_slots = slots_of(anc_grand, anc_grand.shape[1] // n_col)
    root_blocks = per_root * n_col
    is_root = grand_slots < root_blocks
    in_child = grand_slots - root_blocks
    child_block = in_child % (per_child * n_col)
    child_kid = in_child // (per_child * n_col)
    owner = jnp.where(is_root, grand_slots // per_root, child_block // per_child)
    local = jnp.where(is_root, grand_slots % per_root, per_root + child_kid * per_child + child_block % per_child)
    child_owner, owner = child_owner == here, owner == here
    child_tables = by_core(child_owner, cores) + by_core(child_local, cores)
    child_tables = (child_tables[0], child_tables[2], child_tables[1], child_tables[3])
    grand_tables = by_core(owner, cores) + by_core(local, cores)
    grand_tables = (grand_tables[0], grand_tables[2], grand_tables[1], grand_tables[3])
    root_same, child_tables, grand_tables, cores = lax.optimization_barrier(
        (root_same, child_tables, grand_tables, cores)
    )
    own = matmul(root_same.reshape(-1, root_same.shape[2]), inv_root, "si,ij->sj")
    far = matmul(root_other.reshape(-1, root_other.shape[2]), inv_root, "si,ij->sj")
    root_partial = col_join(own.reshape(root_same.shape[:2] + own.shape[1:]), far.reshape(root_other.shape[:2] + far.shape[1:]), cores)
    x_root = exchange_sum(root_partial.reshape((-1,) + root_partial.shape[2:]), "wide")
    x_root, child_tables, grand_tables, cores = lax.optimization_barrier(
        (x_root, child_tables, grand_tables, cores)
    )
    root_tiles = x_root.reshape(x_root.shape[0], per_root, BLK).transpose(1, 0, 2)
    near_local = send_blocks(root_tiles, child_tables)
    near_local = rows_of(near_local, anc_child.shape[0], anc_child.shape[1] // n_col)
    near_rows = exchange_gather(near_local, "wide", 0)
    x_child = level(z_child, near_rows, panel_child, "ska,kaj->skj", inv_child, cores)

    x_child, grand_tables, cores = lax.optimization_barrier((x_child, grand_tables, cores))
    child_tiles = x_child.reshape(x_child.shape[0], kids * per_child, BLK).transpose(1, 0, 2)
    all_tiles = jnp.concatenate([root_tiles, child_tiles], axis=0)
    far_local = send_blocks(all_tiles, grand_tables)
    far_local = rows_of(far_local, anc_grand.shape[0], anc_grand.shape[1] // n_col)
    far_rows = exchange_gather(far_local, "wide", 0)
    x_grand = level(z_grand, far_rows, panel_grand, "sga,gaj->sgj", inv_grand, cores)
    return (x_root, x_child, x_grand)


def solution(mesh):
    in_specs = (
        P("col", "wide"),
        P("col", None, "wide"),
        P("col", None, "wide"),
        P("wide", "col"),
        P(None, "wide", "col"),
        P(None, "wide", "col"),
        P(None, "col", "wide"),
        P(None, "col", "wide"),
        P(None, "col"),
        P(None, "col"),
    )
    out_specs = (P("wide", "col"), P("wide", None, "col"), P("wide", None, "col"))
    return jax.shard_map(
        per_device, mesh=mesh, in_specs=in_specs, out_specs=out_specs, check_vma=False
    )
```
